32 devices in a mesh: pix: 16 (over z, y, x), mode: 2 (over core).
Axes of the slice: x: 2, y: 2, z: 4, core: 2. Of those that a mesh axis runs over, the one named last changes fastest.
Arguments:
- frames: float32 [384, 49152], P('mode', 'pix'), may hold values from -40 to 40
- basis: float32 [2048, 49152], P('mode', 'pix'), may hold values from -0.078125 to 0.078125
- annulus: int32 [64], P('pix'), may hold values from 0 to 7, as said below
- truncation: int32 [8], replicated, may hold values from 256 to 2048
Outputs:
- residual: float32 [384, 49152], P('mode', 'pix')
The draws below stay inside these ranges and needn't reach their ends.
Inputs may be any that keep to these rules, and one draw needn't show every extreme that they name: Every annulus holds one block or more; the blocks of an annulus may lie anywhere in the image.
All inputs are finite; a program needn't handle non-finite values.
Results may differ from the reference program's by a relative error of at most 0.0001.
Values sent between devices are 32-bit elements; how exact they have to be, the bound alone decides.
No kernel may reach another device: no remote copies, remote signals or barrier semaphores. Data moves between devices by JAX's collectives and lax.ppermute only.
A program may use at most 128 MiB of HBM per device.

```python
import math
import jax
import jax.numpy as jnp
from jax import lax

K = 2048
NF = 384
NA = 8
NBLK = 64
PIXELS = 49152
N_MODE = 2


def draw_frames(key, part):
    noise_key, amp_key, scale_key, phase_key = jax.random.split(key, 4)
    position = jnp.arange(PIXELS, dtype=jnp.float32) / PIXELS
    phase = jax.random.uniform(phase_key, (NF, 1), jnp.float32, -math.pi, math.pi)
    noise = jnp.clip(jax.random.normal(noise_key, (NF, PIXELS), jnp.float32), -6.0, 6.0)
    scale = jnp.exp(jax.random.uniform(scale_key, (NF, 1), jnp.float32, math.log(0.5), math.log(5.0)))
    amplitude = jax.random.uniform(amp_key, (NF, 1), jnp.float32, 0.5, 2.0)
    background = amplitude * (1.0 + 2.0 * position[None, :]) * (1.0 + 0.5 * jnp.cos(2.0 * math.pi * 7.0 * position[None, :] + phase))
    return (scale * noise + background).astype(jnp.float32)


def draw_annulus(key, part):
    label_key, order_key = jax.random.split(jax.random.fold_in(key, 17), 2)
    first = jnp.arange(NA, dtype=jnp.int32)
    others = jax.random.randint(label_key, (NBLK - NA,), 0, NA, dtype=jnp.int32)
    labels = jnp.concatenate([first, others])
    order = jax.random.permutation(order_key, NBLK)
    return labels[order].astype(jnp.int32)


def plant(result, stream_key, low, largest):
    spot = [jax.random.randint(jax.random.fold_in(stream_key, axis), (), 0, length) for axis, length in enumerate(result.shape)]
    main_axis = result.shape.index(max(result.shape))
    neighbour = spot[:main_axis] + [(spot[main_axis] + 1) % result.shape[main_axis]] + spot[main_axis + 1:]
    return result.at[tuple(spot)].set(low).at[tuple(neighbour)].set(largest)


def level_of(stream_key, extent, cuts, least, largest):
    level, own = 1.0, jax.random.fold_in(stream_key, 6)
    for dim, parts in cuts:
        steps = jnp.exp(jax.random.uniform(jax.random.fold_in(own, dim), (parts,), jnp.float32, least / len(cuts), largest / len(cuts)))
        level = level * jnp.repeat(steps, extent[dim] // parts).reshape([-1 if axis == dim else 1 for axis in range(len(extent))])
    return level


def gaussian(rng, extent, deviation, limit, shards=(), held_as=jnp.bfloat16):
    array = deviation * jax.random.normal(rng, extent, jnp.float32)
    if shards:
        array = array * level_of(rng, extent, shards, -0.22, 0.18)
    return jnp.clip(array, -limit, limit).astype(held_as)


def setup_inputs(seed: int = 0) -> dict:
    arg_keys = jax.random.split(jax.random.key(seed), 5)
    return {
        "frames": draw_frames(jax.random.fold_in(arg_keys[4], 71), 0),
        "basis": gaussian(arg_keys[1], (K, PIXELS), (PIXELS // NA) ** -0.5, 0.078125, ((0, 2), (1, 16)), jnp.float32),
        "annulus": draw_annulus(jax.random.fold_in(arg_keys[4], 71), 0),
        "truncation": plant(jax.random.randint(arg_keys[3], (NA,), K // 8, K + 1), jax.random.fold_in(arg_keys[3], 1), K // 8, K).astype(jnp.int32),
    }


HIGHEST_PRECISION = lax.Precision.HIGHEST


def reference(frames, basis, annulus, truncation):
    block_count = annulus.shape[0]
    block_len = frames.shape[1] // block_count
    modes_group = K // N_MODE
    onehot = (annulus[:, None] == jnp.arange(NA, dtype=jnp.int32)[None, :]).astype(jnp.float32)
    framed = frames.reshape(NF, block_count, block_len)
    shaped = basis.reshape(K, block_count, block_len)
    pixel_counts = jnp.sum(onehot, axis=0) * block_len
    annulus_sums = jnp.einsum('ba,fb->af', onehot, jnp.sum(framed, axis=2), precision=HIGHEST_PRECISION)
    annulus_means = annulus_sums / pixel_counts[:, None]
    centered = framed - jnp.einsum('ba,af->fb', onehot, annulus_means, precision=HIGHEST_PRECISION)[:, :, None]

    def add_block(running, block_index):
        block_part = jnp.dot(centered[:, block_index, :], shaped[:, block_index, :].T, precision=HIGHEST_PRECISION)
        return running + onehot[block_index][:, None, None] * block_part[None, :, :], None

    coefficients, _ = lax.scan(add_block, jnp.zeros((NA, NF, K), jnp.float32), jnp.arange(block_count, dtype=jnp.int32))
    retained = (jnp.arange(K, dtype=jnp.int32)[None, :] < truncation[:, None]).astype(jnp.float32)
    truncated = coefficients * retained[:, None, :]

    def model_block(block_index):
        picked = jnp.tensordot(onehot[block_index], truncated, axes=1, precision=HIGHEST_PRECISION)
        grouped = picked.reshape(NF, N_MODE, modes_group)
        pieces = shaped[:, block_index, :].reshape(N_MODE, modes_group, block_len)
        partials = jnp.einsum('fmk,mkp->mfp', grouped, pieces, precision=HIGHEST_PRECISION)
        return jnp.sum(partials, axis=0)

    models = lax.map(model_block, jnp.arange(block_count, dtype=jnp.int32))
    residual = centered - jnp.transpose(models, (1, 0, 2))
    return residual.reshape(NF, block_count * block_len)
```

```python
import jax
import jax.numpy as jnp
from jax import lax
from jax.sharding import PartitionSpec as P

NA = 8


HIGHEST_PRECISION = lax.Precision.HIGHEST


def block_products(source, shaped, onehot):
    per_block = jnp.einsum("fbp,kbp->bfk", source, shaped, precision=HIGHEST_PRECISION)
    return jnp.einsum("ba,bfk->afk", onehot, per_block, precision=HIGHEST_PRECISION)


def butterfly_sum(value, axis):
    size = lax.axis_size(axis)
    step = 1
    while step < size:
        pairs = [(i, i ^ step) for i in range(size)]
        value = value + lax.ppermute(value, axis, pairs)
        step *= 2
    return value


def local(frames, basis, annulus, truncation):
    gathered = lax.all_gather(frames, "mode", axis=0, tiled=True)
    total_frames, pix_dev = gathered.shape
    own_rows = frames.shape[0]
    blocks = annulus.shape[0]
    block_len = pix_dev // blocks
    modes_dev = basis.shape[0]
    onehot = (annulus[:, None] == jnp.arange(NA, dtype=jnp.int32)[None, :]).astype(jnp.float32)
    framed = gathered.reshape(total_frames, blocks, block_len)
    shaped = basis.reshape(modes_dev, blocks, block_len)
    local_sums = jnp.einsum(
        "ba,fb->af", onehot, jnp.sum(framed, axis=2), precision=HIGHEST_PRECISION
    )
    local_counts = jnp.sum(onehot, axis=0) * block_len
    mode_ids = lax.axis_index("mode") * modes_dev + jnp.arange(modes_dev, dtype=jnp.int32)
    retained = (mode_ids[None, :] < truncation[:, None]).astype(jnp.float32)
    packed = butterfly_sum(jnp.concatenate([local_sums, local_counts[:, None]], axis=1), "pix")
    annulus_totals, pixel_counts = packed[:, :-1], packed[:, -1]
    annulus_means = annulus_totals / pixel_counts[:, None]
    centered = (
        framed
        - jnp.einsum("ba,af->fb", onehot, annulus_means, precision=HIGHEST_PRECISION)[:, :, None]
    )
    partial_value = block_products(centered, shaped, onehot)
    coefficients = lax.psum(partial_value, "pix")
    truncated = coefficients * retained[:, None, :]
    picked = jnp.einsum("ba,afk->bfk", onehot, truncated, precision=HIGHEST_PRECISION)
    term = jnp.einsum("bfk,kbp->fbp", picked, shaped, precision=HIGHEST_PRECISION)
    model_rows = lax.psum_scatter(
        term.reshape(own_rows * lax.axis_size("mode"), pix_dev),
        "mode",
        scatter_dimension=0,
        tiled=True,
    )
    own_means = lax.dynamic_slice_in_dim(
        annulus_means, lax.axis_index("mode") * own_rows, own_rows, 1
    )
    own_frames = frames.reshape(own_rows, blocks, block_len)
    own_centered = (
        own_frames
        - jnp.einsum("ba,af->fb", onehot, own_means, precision=HIGHEST_PRECISION)[:, :, None]
    )
    return (own_centered - model_rows.reshape(own_rows, blocks, block_len)).reshape(
        own_rows, pix_dev
    )


def solution(mesh):
    return jax.shard_map(
        local,
        mesh=mesh,
        in_specs=(P("mode", "pix"), P("mode", "pix"), P("pix"), P()),
        out_specs=P("mode", "pix"),
        check_vma=False,
    )
```

```python
import jax
import jax.numpy as jnp
from jax import lax
from jax.sharding import PartitionSpec as P

NA = 8


HIGHEST_PRECISION = lax.Precision.HIGHEST


def block_products(source, shaped, onehot):
    per_block = jnp.einsum("fbp,kbp->bfk", source, shaped, precision=HIGHEST_PRECISION)
    return jnp.einsum("ba,bfk->afk", onehot, per_block, precision=HIGHEST_PRECISION)


def butterfly_sum(value, axis):
    size = lax.axis_size(axis)
    step = 1
    while step < size:
        pairs = [(i, i ^ step) for i in range(size)]
        value = value + lax.ppermute(value, axis, pairs)
        step *= 2
    return value


def local(frames, basis, annulus, truncation):
    gathered = lax.all_gather(frames, "mode", axis=0, tiled=True)
    total_frames, pix_dev = gathered.shape
    own_rows = frames.shape[0]
    blocks = annulus.shape[0]
    block_len = pix_dev // blocks
    modes_dev = basis.shape[0]
    onehot = (annulus[:, None] == jnp.arange(NA, dtype=jnp.int32)[None, :]).astype(jnp.float32)
    framed = gathered.reshape(total_frames, blocks, block_len)
    shaped = basis.reshape(modes_dev, blocks, block_len)
    local_sums = jnp.einsum(
        "ba,fb->af", onehot, jnp.sum(framed, axis=2), precision=HIGHEST_PRECISION
    )
    local_counts = jnp.sum(onehot, axis=0) * block_len
    mode_ids = lax.axis_index("mode") * modes_dev + jnp.arange(modes_dev, dtype=jnp.int32)
    retained = (mode_ids[None, :] < truncation[:, None]).astype(jnp.float32)
    packed = butterfly_sum(jnp.concatenate([local_sums, local_counts[:, None]], axis=1), "pix")
    annulus_totals, pixel_counts = packed[:, :-1], packed[:, -1]
    annulus_means = annulus_totals / pixel_counts[:, None]
    centered = (
        framed
        - jnp.einsum("ba,af->fb", onehot, annulus_means, precision=HIGHEST_PRECISION)[:, :, None]
    )
    per_block = jnp.einsum("fbp,kbp->bfk", centered, shaped, precision=HIGHEST_PRECISION)
    gathered_blocks = lax.all_to_all(per_block, "pix", 1, 0, tiled=True)
    every_annulus = lax.all_gather(annulus, "pix", axis=0, tiled=True)
    every_onehot = (every_annulus[:, None] == jnp.arange(NA, dtype=jnp.int32)[None, :]).astype(
        jnp.float32
    )
    slice_coefficients = jnp.einsum(
        "ba,bfk->afk", every_onehot, gathered_blocks, precision=HIGHEST_PRECISION
    )
    slice_truncated = slice_coefficients * retained[:, None, :]
    outgoing = jnp.take(slice_truncated, every_annulus, axis=0)
    picked = lax.all_to_all(outgoing, "pix", 0, 1, tiled=True)
    term = jnp.einsum("bfk,kbp->fbp", picked, shaped, precision=HIGHEST_PRECISION)
    model_rows = lax.psum_scatter(
        term.reshape(own_rows * lax.axis_size("mode"), pix_dev),
        "mode",
        scatter_dimension=0,
        tiled=True,
    )
    own_means = lax.dynamic_slice_in_dim(
        annulus_means, lax.axis_index("mode") * own_rows, own_rows, 1
    )
    own_frames = frames.reshape(own_rows, blocks, block_len)
    own_centered = (
        own_frames
        - jnp.einsum("ba,af->fb", onehot, own_means, precision=HIGHEST_PRECISION)[:, :, None]
    )
    return (own_centered - model_rows.reshape(own_rows, blocks, block_len)).reshape(
        own_rows, pix_dev
    )


def solution(mesh):
    return jax.shard_map(
        local,
        mesh=mesh,
        in_specs=(P("mode", "pix"), P("mode", "pix"), P("pix"), P()),
        out_specs=P("mode", "pix"),
        check_vma=False,
    )
```

```python
import jax
import jax.numpy as jnp
from jax import lax
from jax.sharding import PartitionSpec as P

NA = 8
K_CHUNKS = 2


HIGHEST_PRECISION = lax.Precision.HIGHEST


def butterfly_sum(value, axis):
    size = lax.axis_size(axis)
    step = 1
    while step < size:
        pairs = [(i, i ^ step) for i in range(size)]
        value = value + lax.ppermute(value, axis, pairs)
        step *= 2
    return value


def local(frames, basis, annulus, truncation):
    gathered = lax.all_gather(frames, "mode", axis=0, tiled=True)
    total_frames, pix_dev = gathered.shape
    own_rows = frames.shape[0]
    blocks = annulus.shape[0]
    block_len = pix_dev // blocks
    modes_dev = basis.shape[0]
    parts = lax.axis_size("pix")
    onehot = (annulus[:, None] == jnp.arange(NA, dtype=jnp.int32)[None, :]).astype(jnp.float32)
    framed = gathered.reshape(total_frames, blocks, block_len)
    shaped = basis.reshape(modes_dev, blocks, block_len)
    local_sums = jnp.einsum(
        "ba,fb->af", onehot, jnp.sum(framed, axis=2), precision=HIGHEST_PRECISION
    )
    local_counts = jnp.sum(onehot, axis=0) * block_len
    own_slot = (
        lax.axis_index("pix") * blocks + jnp.arange(blocks, dtype=jnp.int32)
    )[:, None] == jnp.arange(parts * blocks, dtype=jnp.int32)[None, :]
    local_table = jnp.einsum(
        "ba,bc->ac", onehot, own_slot.astype(jnp.float32), precision=HIGHEST_PRECISION
    )
    packed = butterfly_sum(
        jnp.concatenate([local_sums, local_counts[:, None], local_table], axis=1), "pix"
    )
    annulus_totals = packed[:, :total_frames]
    pixel_counts = packed[:, total_frames]
    every_onehot = packed[:, total_frames + 1 :].T
    every_annulus = jnp.einsum(
        "ba,a->b", every_onehot, jnp.arange(NA, dtype=jnp.float32), precision=HIGHEST_PRECISION
    ).astype(jnp.int32)
    mode_ids = lax.axis_index("mode") * modes_dev + jnp.arange(modes_dev, dtype=jnp.int32)
    retained = (mode_ids[None, :] < truncation[:, None]).astype(jnp.float32)
    annulus_means = annulus_totals / pixel_counts[:, None]
    centered = (
        framed
        - jnp.einsum("ba,af->fb", onehot, annulus_means, precision=HIGHEST_PRECISION)[:, :, None]
    )
    chunk = modes_dev // K_CHUNKS
    term = None
    for c in range(K_CHUNKS):
        piece = shaped[c * chunk : (c + 1) * chunk]
        per_block = jnp.einsum("fbp,kbp->bfk", centered, piece, precision=HIGHEST_PRECISION)
        gathered_blocks = lax.all_to_all(per_block, "pix", 1, 0, tiled=True)
        slice_coefficients = jnp.einsum(
            "ba,bfk->afk", every_onehot, gathered_blocks, precision=HIGHEST_PRECISION
        )
        slice_truncated = slice_coefficients * retained[:, None, c * chunk : (c + 1) * chunk]
        outgoing = jnp.take(slice_truncated, every_annulus, axis=0)
        picked = lax.all_to_all(outgoing, "pix", 0, 1, tiled=True)
        part = jnp.einsum("bfk,kbp->fbp", picked, piece, precision=HIGHEST_PRECISION)
        term = part if term is None else term + part
    model_rows = lax.psum_scatter(
        term.reshape(own_rows * lax.axis_size("mode"), pix_dev),
        "mode",
        scatter_dimension=0,
        tiled=True,
    )
    own_means = lax.dynamic_slice_in_dim(
        annulus_means, lax.axis_index("mode") * own_rows, own_rows, 1
    )
    own_frames = frames.reshape(own_rows, blocks, block_len)
    own_centered = (
        own_frames
        - jnp.einsum("ba,af->fb", onehot, own_means, precision=HIGHEST_PRECISION)[:, :, None]
    )
    return (own_centered - model_rows.reshape(own_rows, blocks, block_len)).reshape(
        own_rows, pix_dev
    )


def solution(mesh):
    return jax.shard_map(
        local,
        mesh=mesh,
        in_specs=(P("mode", "pix"), P("mode", "pix"), P("pix"), P()),
        out_specs=P("mode", "pix"),
        check_vma=False,
    )
```

```python
import jax
import jax.numpy as jnp
from jax import lax
from jax.sharding import PartitionSpec as P

NA = 8
K_CHUNKS = 2


HIGHEST_PRECISION = lax.Precision.HIGHEST


def butterfly_sum(value, axes, size):
    step = 1
    while step < size:
        pairs = [(i, i ^ step) for i in range(size)]
        value = value + lax.ppermute(value, axes, pairs)
        step *= 2
    return value


def local(frames, basis, annulus, truncation):
    own_rows, pix_dev = frames.shape
    groups = lax.axis_size("mode")
    parts = lax.axis_size("pix")
    total_frames = own_rows * groups
    blocks = annulus.shape[0]
    block_len = pix_dev // blocks
    modes_dev = basis.shape[0]
    gathered = lax.all_gather(frames, "mode", axis=0, tiled=True)
    mode_index = lax.axis_index("mode")
    onehot = (annulus[:, None] == jnp.arange(NA, dtype=jnp.int32)[None, :]).astype(jnp.float32)
    own_block_sums = jnp.stack(
        [jnp.sum(frames[:, b * block_len : (b + 1) * block_len], axis=1) for b in range(blocks)],
        axis=0,
    )
    own_sums = jnp.einsum("ba,bf->af", onehot, own_block_sums, precision=HIGHEST_PRECISION)
    frame_slot = (
        mode_index * own_rows + jnp.arange(own_rows, dtype=jnp.int32)
    )[:, None] == jnp.arange(total_frames, dtype=jnp.int32)[None, :]
    local_sums = jnp.einsum(
        "af,fg->ag", own_sums, frame_slot.astype(jnp.float32), precision=HIGHEST_PRECISION
    )
    first_group = (mode_index == 0).astype(jnp.float32)
    local_counts = jnp.sum(onehot, axis=0) * (block_len * first_group)
    own_slot = (
        lax.axis_index("pix") * blocks + jnp.arange(blocks, dtype=jnp.int32)
    )[:, None] == jnp.arange(parts * blocks, dtype=jnp.int32)[None, :]
    local_table = jnp.einsum(
        "ba,bc->ac", onehot, own_slot.astype(jnp.float32), precision=HIGHEST_PRECISION
    ) * first_group
    packed = butterfly_sum(
        jnp.concatenate([local_sums, local_counts[:, None], local_table], axis=1),
        ("pix", "mode"),
        parts * groups,
    )
    annulus_totals = packed[:, :total_frames]
    pixel_counts = packed[:, total_frames]
    every_onehot = packed[:, total_frames + 1 :].T
    every_annulus = jnp.einsum(
        "ba,a->b", every_onehot, jnp.arange(NA, dtype=jnp.float32), precision=HIGHEST_PRECISION
    ).astype(jnp.int32)
    mode_ids = mode_index * modes_dev + jnp.arange(modes_dev, dtype=jnp.int32)
    retained = (mode_ids[None, :] < truncation[:, None]).astype(jnp.float32)
    annulus_means = annulus_totals / pixel_counts[:, None]
    block_means = jnp.einsum("ba,af->bf", onehot, annulus_means, precision=HIGHEST_PRECISION)
    centered = [
        gathered[:, b * block_len : (b + 1) * block_len] - block_means[b][:, None]
        for b in range(blocks)
    ]
    chunk = modes_dev // K_CHUNKS
    term = None
    for c in range(K_CHUNKS):
        pieces = [
            basis[c * chunk : (c + 1) * chunk, b * block_len : (b + 1) * block_len]
            for b in range(blocks)
        ]
        per_block = jnp.stack(
            [
                jnp.dot(centered[b], pieces[b].T, precision=HIGHEST_PRECISION)
                for b in range(blocks)
            ],
            axis=0,
        )
        gathered_blocks = lax.all_to_all(per_block, "pix", 1, 0, tiled=True)
        slice_coefficients = jnp.einsum(
            "ba,bfk->afk", every_onehot, gathered_blocks, precision=HIGHEST_PRECISION
        )
        slice_truncated = slice_coefficients * retained[:, None, c * chunk : (c + 1) * chunk]
        outgoing = jnp.take(slice_truncated, every_annulus, axis=0)
        picked = lax.all_to_all(outgoing, "pix", 0, 1, tiled=True)
        part = jnp.concatenate(
            [jnp.dot(picked[b], pieces[b], precision=HIGHEST_PRECISION) for b in range(blocks)],
            axis=1,
        )
        term = part if term is None else term + part
    model_rows = lax.psum_scatter(term, "mode", scatter_dimension=0, tiled=True)
    own_means = lax.dynamic_slice_in_dim(block_means, mode_index * own_rows, own_rows, 1)
    own_centered = jnp.concatenate(
        [
            frames[:, b * block_len : (b + 1) * block_len] - own_means[b][:, None]
            for b in range(blocks)
        ],
        axis=1,
    )
    return own_centered - model_rows


def solution(mesh):
    return jax.shard_map(
        local,
        mesh=mesh,
        in_specs=(P("mode", "pix"), P("mode", "pix"), P("pix"), P()),
        out_specs=P("mode", "pix"),
        check_vma=False,
    )
```

```python
import jax
import jax.numpy as jnp
from jax import lax
from jax.sharding import PartitionSpec as P

NA = 8
K_CHUNKS = 2


HIGHEST_PRECISION = lax.Precision.HIGHEST


def butterfly_sum(value, axes, size):
    step = 1
    while step < size:
        pairs = [(i, i ^ step) for i in range(size)]
        value = value + lax.ppermute(value, axes, pairs)
        step *= 2
    return value


def local(frames, basis, annulus, truncation):
    own_rows, pix_dev = frames.shape
    groups = lax.axis_size("mode")
    parts = lax.axis_size("pix")
    total_frames = own_rows * groups
    blocks = annulus.shape[0]
    block_len = pix_dev // blocks
    modes_dev = basis.shape[0]
    gathered = lax.all_gather(frames, "mode", axis=0, tiled=True)
    mode_index = lax.axis_index("mode")
    onehot = (annulus[:, None] == jnp.arange(NA, dtype=jnp.int32)[None, :]).astype(jnp.float32)
    own_block_sums = jnp.stack(
        [jnp.sum(frames[:, b * block_len : (b + 1) * block_len], axis=1) for b in range(blocks)],
        axis=0,
    )
    own_sums = jnp.einsum("ba,bf->af", onehot, own_block_sums, precision=HIGHEST_PRECISION)
    frame_slot = (
        mode_index * own_rows + jnp.arange(own_rows, dtype=jnp.int32)
    )[:, None] == jnp.arange(total_frames, dtype=jnp.int32)[None, :]
    local_sums = jnp.einsum(
        "af,fg->ag", own_sums, frame_slot.astype(jnp.float32), precision=HIGHEST_PRECISION
    )
    first_group = (mode_index == 0).astype(jnp.float32)
    local_counts = jnp.sum(onehot, axis=0) * (block_len * first_group)
    own_slot = (
        lax.axis_index("pix") * blocks + jnp.arange(blocks, dtype=jnp.int32)
    )[:, None] == jnp.arange(parts * blocks, dtype=jnp.int32)[None, :]
    local_table = jnp.einsum(
        "ba,bc->ac", onehot, own_slot.astype(jnp.float32), precision=HIGHEST_PRECISION
    ) * first_group
    packed = butterfly_sum(
        jnp.concatenate([local_sums, local_counts[:, None], local_table], axis=1),
        ("pix", "mode"),
        parts * groups,
    )
    annulus_totals = packed[:, :total_frames]
    pixel_counts = packed[:, total_frames]
    every_onehot = packed[:, total_frames + 1 :].T
    every_annulus = jnp.einsum(
        "ba,a->b", every_onehot, jnp.arange(NA, dtype=jnp.float32), precision=HIGHEST_PRECISION
    ).astype(jnp.int32)
    mode_ids = mode_index * modes_dev + jnp.arange(modes_dev, dtype=jnp.int32)
    retained = (mode_ids[None, :] < truncation[:, None]).astype(jnp.float32)
    annulus_means = annulus_totals / pixel_counts[:, None]
    block_means = jnp.einsum("ba,af->bf", onehot, annulus_means, precision=HIGHEST_PRECISION)
    centered = [
        gathered[:, b * block_len : (b + 1) * block_len] - block_means[b][:, None]
        for b in range(blocks)
    ]
    chunk = modes_dev // K_CHUNKS
    rows_dev = total_frames // parts
    pieces = [
        [
            basis[c * chunk : (c + 1) * chunk, b * block_len : (b + 1) * block_len]
            for b in range(blocks)
        ]
        for c in range(K_CHUNKS)
    ]

    def outbound(c):
        per_block = jnp.stack(
            [
                jnp.dot(centered[b], pieces[c][b].T, precision=HIGHEST_PRECISION)
                for b in range(blocks)
            ],
            axis=0,
        )
        return per_block.reshape(blocks, parts, rows_dev, chunk).transpose(1, 0, 2, 3)

    def inbound(c, arrived):
        slice_coefficients = jnp.einsum(
            "ba,bfk->afk",
            every_onehot,
            arrived.reshape(parts * blocks, rows_dev, chunk),
            precision=HIGHEST_PRECISION,
        )
        slice_truncated = slice_coefficients * retained[:, None, c * chunk : (c + 1) * chunk]
        outgoing = jnp.take(slice_truncated, every_annulus, axis=0)
        return outgoing.reshape(parts, blocks, rows_dev, chunk)

    def model_of(c, returned):
        picked = returned.transpose(1, 0, 2, 3).reshape(blocks, total_frames, chunk)
        return jnp.concatenate(
            [jnp.dot(picked[b], pieces[c][b], precision=HIGHEST_PRECISION) for b in range(blocks)],
            axis=1,
        )

    term = None
    pending = None
    for stage in range(K_CHUNKS + 1):
        sending = []
        if stage < K_CHUNKS:
            sending.append(outbound(stage))
        if pending is not None:
            sending.append(pending)
        received = lax.all_to_all(jnp.stack(sending, axis=1), "pix", 0, 0, tiled=True)
        slot = 0
        next_pending = None
        if stage < K_CHUNKS:
            next_pending = inbound(stage, received[:, 0])
            slot = 1
        if pending is not None:
            part = model_of(stage - 1, received[:, slot])
            term = part if term is None else term + part
        pending = next_pending
    model_rows = lax.psum_scatter(term, "mode", scatter_dimension=0, tiled=True)
    own_means = lax.dynamic_slice_in_dim(block_means, mode_index * own_rows, own_rows, 1)
    own_centered = jnp.concatenate(
        [
            frames[:, b * block_len : (b + 1) * block_len] - own_means[b][:, None]
            for b in range(blocks)
        ],
        axis=1,
    )
    return own_centered - model_rows


def solution(mesh):
    return jax.shard_map(
        local,
        mesh=mesh,
        in_specs=(P("mode", "pix"), P("mode", "pix"), P("pix"), P()),
        out_specs=P("mode", "pix"),
        check_vma=False,
    )
```

```python
import jax
import jax.numpy as jnp
from jax import lax
from jax.sharding import PartitionSpec as P

NA = 8
K_CHUNKS = 2


HIGHEST_PRECISION = lax.Precision.HIGHEST


def butterfly_sum(value, axes, size):
    step = 1
    while step < size:
        pairs = [(i, i ^ step) for i in range(size)]
        value = value + lax.ppermute(value, axes, pairs)
        step *= 2
    return value


def local(frames, basis, annulus, truncation):
    own_rows, pix_dev = frames.shape
    groups = lax.axis_size("mode")
    parts = lax.axis_size("pix")
    total_frames = own_rows * groups
    blocks = annulus.shape[0]
    block_len = pix_dev // blocks
    modes_dev = basis.shape[0]
    gathered = lax.all_gather(frames, "mode", axis=0, tiled=True)
    mode_index = lax.axis_index("mode")
    onehot = (annulus[:, None] == jnp.arange(NA, dtype=jnp.int32)[None, :]).astype(jnp.float32)
    own_block_sums = jnp.stack(
        [jnp.sum(frames[:, b * block_len : (b + 1) * block_len], axis=1) for b in range(blocks)],
        axis=0,
    )
    own_sums = jnp.einsum("ba,bf->af", onehot, own_block_sums, precision=HIGHEST_PRECISION)
    frame_slot = (
        mode_index * own_rows + jnp.arange(own_rows, dtype=jnp.int32)
    )[:, None] == jnp.arange(total_frames, dtype=jnp.int32)[None, :]
    local_sums = jnp.einsum(
        "af,fg->ag", own_sums, frame_slot.astype(jnp.float32), precision=HIGHEST_PRECISION
    )
    first_group = (mode_index == 0).astype(jnp.float32)
    local_counts = jnp.sum(onehot, axis=0) * (block_len * first_group)
    own_slot = (
        lax.axis_index("pix") * blocks + jnp.arange(blocks, dtype=jnp.int32)
    )[:, None] == jnp.arange(parts * blocks, dtype=jnp.int32)[None, :]
    local_table = jnp.einsum(
        "ba,bc->ac", onehot, own_slot.astype(jnp.float32), precision=HIGHEST_PRECISION
    ) * first_group
    packed = butterfly_sum(
        jnp.concatenate([local_sums, local_counts[:, None], local_table], axis=1),
        ("pix", "mode"),
        parts * groups,
    )
    annulus_totals = packed[:, :total_frames]
    pixel_counts = packed[:, total_frames]
    every_onehot = packed[:, total_frames + 1 :].T
    mode_ids = mode_index * modes_dev + jnp.arange(modes_dev, dtype=jnp.int32)
    retained = (mode_ids[None, :] < truncation[:, None]).astype(jnp.float32)
    annulus_means = annulus_totals / pixel_counts[:, None]
    block_means = jnp.einsum("ba,af->bf", onehot, annulus_means, precision=HIGHEST_PRECISION)
    centered = [
        gathered[:, b * block_len : (b + 1) * block_len] - block_means[b][:, None]
        for b in range(blocks)
    ]
    chunk = modes_dev // K_CHUNKS
    same_annulus = jnp.einsum("ca,ba->cb", every_onehot, every_onehot, precision=HIGHEST_PRECISION)
    block_retained = jnp.einsum("ba,ak->bk", every_onehot, retained, precision=HIGHEST_PRECISION)
    rows_dev = total_frames // parts
    pieces = [
        [
            basis[c * chunk : (c + 1) * chunk, b * block_len : (b + 1) * block_len]
            for b in range(blocks)
        ]
        for c in range(K_CHUNKS)
    ]

    def outbound(c):
        per_block = jnp.stack(
            [
                jnp.dot(centered[b], pieces[c][b].T, precision=HIGHEST_PRECISION)
                for b in range(blocks)
            ],
            axis=0,
        )
        return per_block.reshape(blocks, parts, rows_dev, chunk).transpose(1, 0, 2, 3)

    def inbound(c, arrived):
        summed = jnp.einsum(
            "cb,bfk->cfk",
            same_annulus,
            arrived.reshape(parts * blocks, rows_dev, chunk),
            precision=HIGHEST_PRECISION,
        )
        outgoing = summed * block_retained[:, None, c * chunk : (c + 1) * chunk]
        return outgoing.reshape(parts, blocks, rows_dev, chunk)

    def model_of(c, returned):
        picked = returned.transpose(1, 0, 2, 3).reshape(blocks, total_frames, chunk)
        return jnp.concatenate(
            [jnp.dot(picked[b], pieces[c][b], precision=HIGHEST_PRECISION) for b in range(blocks)],
            axis=1,
        )

    term = None
    pending = None
    for stage in range(K_CHUNKS + 1):
        sending = []
        if stage < K_CHUNKS:
            sending.append(outbound(stage))
        if pending is not None:
            sending.append(pending)
        received = lax.all_to_all(jnp.stack(sending, axis=1), "pix", 0, 0, tiled=True)
        slot = 0
        next_pending = None
        if stage < K_CHUNKS:
            next_pending = inbound(stage, received[:, 0])
            slot = 1
        if pending is not None:
            part = model_of(stage - 1, received[:, slot])
            term = part if term is None else term + part
        pending = next_pending
    model_rows = lax.psum_scatter(term, "mode", scatter_dimension=0, tiled=True)
    own_means = lax.dynamic_slice_in_dim(block_means, mode_index * own_rows, own_rows, 1)
    own_centered = jnp.concatenate(
        [
            frames[:, b * block_len : (b + 1) * block_len] - own_means[b][:, None]
            for b in range(blocks)
        ],
        axis=1,
    )
    return own_centered - model_rows


def solution(mesh):
    return jax.shard_map(
        local,
        mesh=mesh,
        in_specs=(P("mode", "pix"), P("mode", "pix"), P("pix"), P()),
        out_specs=P("mode", "pix"),
        check_vma=False,
    )
```

```python
import jax
import jax.numpy as jnp
from jax import lax
from jax.sharding import PartitionSpec as P

NA = 8
K_CHUNKS = 2


HIGHEST_PRECISION = lax.Precision.HIGHEST
PRODUCT_PRECISION = lax.Precision.HIGH


def butterfly_sum(value, axes, size):
    step = 1
    while step < size:
        pairs = [(i, i ^ step) for i in range(size)]
        value = value + lax.ppermute(value, axes, pairs)
        step *= 2
    return value


def local(frames, basis, annulus, truncation):
    own_rows, pix_dev = frames.shape
    groups = lax.axis_size("mode")
    parts = lax.axis_size("pix")
    total_frames = own_rows * groups
    blocks = annulus.shape[0]
    block_len = pix_dev // blocks
    modes_dev = basis.shape[0]
    gathered = lax.all_gather(frames, "mode", axis=0, tiled=True)
    mode_index = lax.axis_index("mode")
    onehot = (annulus[:, None] == jnp.arange(NA, dtype=jnp.int32)[None, :]).astype(jnp.float32)
    own_block_sums = jnp.stack(
        [jnp.sum(frames[:, b * block_len : (b + 1) * block_len], axis=1) for b in range(blocks)],
        axis=0,
    )
    own_sums = jnp.einsum("ba,bf->af", onehot, own_block_sums, precision=HIGHEST_PRECISION)
    frame_slot = (
        mode_index * own_rows + jnp.arange(own_rows, dtype=jnp.int32)
    )[:, None] == jnp.arange(total_frames, dtype=jnp.int32)[None, :]
    local_sums = jnp.einsum(
        "af,fg->ag", own_sums, frame_slot.astype(jnp.float32), precision=HIGHEST_PRECISION
    )
    first_group = (mode_index == 0).astype(jnp.float32)
    local_counts = jnp.sum(onehot, axis=0) * (block_len * first_group)
    own_slot = (
        lax.axis_index("pix") * blocks + jnp.arange(blocks, dtype=jnp.int32)
    )[:, None] == jnp.arange(parts * blocks, dtype=jnp.int32)[None, :]
    local_table = jnp.einsum(
        "ba,bc->ac", onehot, own_slot.astype(jnp.float32), precision=HIGHEST_PRECISION
    ) * first_group
    packed = butterfly_sum(
        jnp.concatenate([local_sums, local_counts[:, None], local_table], axis=1),
        ("pix", "mode"),
        parts * groups,
    )
    annulus_totals = packed[:, :total_frames]
    pixel_counts = packed[:, total_frames]
    every_onehot = packed[:, total_frames + 1 :].T
    mode_ids = mode_index * modes_dev + jnp.arange(modes_dev, dtype=jnp.int32)
    retained = (mode_ids[None, :] < truncation[:, None]).astype(jnp.float32)
    annulus_means = annulus_totals / pixel_counts[:, None]
    block_means = jnp.einsum("ba,af->bf", onehot, annulus_means, precision=HIGHEST_PRECISION)
    centered = [
        gathered[:, b * block_len : (b + 1) * block_len] - block_means[b][:, None]
        for b in range(blocks)
    ]
    chunk = modes_dev // K_CHUNKS
    same_annulus = jnp.einsum("ca,ba->cb", every_onehot, every_onehot, precision=HIGHEST_PRECISION)
    block_retained = jnp.einsum("ba,ak->bk", every_onehot, retained, precision=HIGHEST_PRECISION)
    rows_dev = total_frames // parts
    pieces = [
        [
            basis[c * chunk : (c + 1) * chunk, b * block_len : (b + 1) * block_len]
            for b in range(blocks)
        ]
        for c in range(K_CHUNKS)
    ]

    def outbound(c):
        per_block = jnp.stack(
            [
                jnp.dot(centered[b], pieces[c][b].T, precision=PRODUCT_PRECISION)
                for b in range(blocks)
            ],
            axis=0,
        )
        return per_block.reshape(blocks, parts, rows_dev, chunk).transpose(1, 0, 2, 3)

    def inbound(c, arrived):
        summed = jnp.einsum(
            "cb,bfk->cfk",
            same_annulus,
            arrived.reshape(parts * blocks, rows_dev, chunk),
            precision=HIGHEST_PRECISION,
        )
        outgoing = summed * block_retained[:, None, c * chunk : (c + 1) * chunk]
        return outgoing.reshape(parts, blocks, rows_dev, chunk)

    def model_of(c, returned):
        picked = returned.transpose(1, 0, 2, 3).reshape(blocks, total_frames, chunk)
        return jnp.concatenate(
            [jnp.dot(picked[b], pieces[c][b], precision=PRODUCT_PRECISION) for b in range(blocks)],
            axis=1,
        )

    term = None
    pending = None
    for stage in range(K_CHUNKS + 1):
        sending = []
        if stage < K_CHUNKS:
            sending.append(outbound(stage))
        if pending is not None:
            sending.append(pending)
        received = lax.all_to_all(jnp.stack(sending, axis=1), "pix", 0, 0, tiled=True)
        slot = 0
        next_pending = None
        if stage < K_CHUNKS:
            next_pending = inbound(stage, received[:, 0])
            slot = 1
        if pending is not None:
            part = model_of(stage - 1, received[:, slot])
            term = part if term is None else term + part
        pending = next_pending
    model_rows = lax.psum_scatter(term, "mode", scatter_dimension=0, tiled=True)
    own_means = lax.dynamic_slice_in_dim(block_means, mode_index * own_rows, own_rows, 1)
    own_centered = jnp.concatenate(
        [
            frames[:, b * block_len : (b + 1) * block_len] - own_means[b][:, None]
            for b in range(blocks)
        ],
        axis=1,
    )
    return own_centered - model_rows


def solution(mesh):
    return jax.shard_map(
        local,
        mesh=mesh,
        in_specs=(P("mode", "pix"), P("mode", "pix"), P("pix"), P()),
        out_specs=P("mode", "pix"),
        check_vma=False,
    )
```

```python
import jax
import jax.numpy as jnp
from jax import lax
from jax.sharding import PartitionSpec as P

NA = 8


HIGHEST_PRECISION = lax.Precision.HIGHEST
PRODUCT_PRECISION = lax.Precision.HIGH


def butterfly_sum(value, axes, size):
    step = 1
    while step < size:
        pairs = [(i, i ^ step) for i in range(size)]
        value = value + lax.ppermute(value, axes, pairs)
        step *= 2
    return value


def local(frames, basis, annulus, truncation):
    own_rows, pix_dev = frames.shape
    groups = lax.axis_size("mode")
    parts = lax.axis_size("pix")
    total_frames = own_rows * groups
    blocks = annulus.shape[0]
    block_len = pix_dev // blocks
    modes_dev = basis.shape[0]
    gathered = lax.all_gather(frames, "mode", axis=0, tiled=True)
    mode_index = lax.axis_index("mode")
    onehot = (annulus[:, None] == jnp.arange(NA, dtype=jnp.int32)[None, :]).astype(jnp.float32)
    own_block_sums = jnp.stack(
        [jnp.sum(frames[:, b * block_len : (b + 1) * block_len], axis=1) for b in range(blocks)],
        axis=0,
    )
    own_sums = jnp.einsum("ba,bf->af", onehot, own_block_sums, precision=HIGHEST_PRECISION)
    frame_slot = (
        mode_index * own_rows + jnp.arange(own_rows, dtype=jnp.int32)
    )[:, None] == jnp.arange(total_frames, dtype=jnp.int32)[None, :]
    local_sums = jnp.einsum(
        "af,fg->ag", own_sums, frame_slot.astype(jnp.float32), precision=HIGHEST_PRECISION
    )
    first_group = (mode_index == 0).astype(jnp.float32)
    local_counts = jnp.sum(onehot, axis=0) * (block_len * first_group)
    own_slot = (
        lax.axis_index("pix") * blocks + jnp.arange(blocks, dtype=jnp.int32)
    )[:, None] == jnp.arange(parts * blocks, dtype=jnp.int32)[None, :]
    local_table = jnp.einsum(
        "ba,bc->ac", onehot, own_slot.astype(jnp.float32), precision=HIGHEST_PRECISION
    ) * first_group
    packed = butterfly_sum(
        jnp.concatenate([local_sums, local_counts[:, None], local_table], axis=1),
        ("pix", "mode"),
        parts * groups,
    )
    annulus_totals = packed[:, :total_frames]
    pixel_counts = packed[:, total_frames]
    every_onehot = packed[:, total_frames + 1 :].T
    mode_ids = mode_index * modes_dev + jnp.arange(modes_dev, dtype=jnp.int32)
    retained = (mode_ids[None, :] < truncation[:, None]).astype(jnp.float32)
    annulus_means = annulus_totals / pixel_counts[:, None]
    block_means = jnp.einsum("ba,af->bf", onehot, annulus_means, precision=HIGHEST_PRECISION)
    centered = [
        gathered[:, b * block_len : (b + 1) * block_len] - block_means[b][:, None]
        for b in range(blocks)
    ]
    same_annulus = jnp.einsum("ca,ba->cb", every_onehot, every_onehot, precision=HIGHEST_PRECISION)
    block_retained = jnp.einsum("ba,ak->bk", every_onehot, retained, precision=HIGHEST_PRECISION)
    rows_dev = total_frames // parts
    last = modes_dev // 4
    bounds = [(0, modes_dev - last), (modes_dev - last, modes_dev)]
    pieces = [
        [basis[lo:hi, b * block_len : (b + 1) * block_len] for b in range(blocks)]
        for lo, hi in bounds
    ]
    last_basis = lax.all_gather(basis[modes_dev - last :], "mode", axis=0, tiled=True).reshape(
        groups, last, pix_dev
    )

    def outbound(c):
        width = bounds[c][1] - bounds[c][0]
        per_block = jnp.stack(
            [
                jnp.dot(centered[b], pieces[c][b].T, precision=PRODUCT_PRECISION)
                for b in range(blocks)
            ],
            axis=0,
        )
        return per_block.reshape(blocks, parts, rows_dev, width).transpose(1, 0, 2, 3)

    def inbound(c, arrived):
        lo, hi = bounds[c]
        summed = jnp.einsum(
            "cb,bfk->cfk",
            same_annulus,
            arrived.reshape(parts * blocks, rows_dev, hi - lo),
            precision=HIGHEST_PRECISION,
        )
        outgoing = summed * block_retained[:, None, lo:hi]
        return outgoing.reshape(parts, blocks, rows_dev, hi - lo)

    def picked_of(c, returned):
        width = bounds[c][1] - bounds[c][0]
        return returned.transpose(1, 0, 2, 3).reshape(blocks, total_frames, width)

    first_out = outbound(0)
    arrived = lax.all_to_all(first_out, "pix", 0, 0, tiled=True)
    pending = inbound(0, arrived)
    second_out = outbound(1)
    split = bounds[1][1] - bounds[1][0]
    received = lax.all_to_all(
        jnp.concatenate([second_out, pending], axis=3), "pix", 0, 0, tiled=True
    )
    pending = inbound(1, received[..., :split])
    picked = picked_of(0, received[..., split:])
    term = jnp.concatenate(
        [jnp.dot(picked[b], pieces[0][b], precision=PRODUCT_PRECISION) for b in range(blocks)],
        axis=1,
    )
    model_rows = lax.psum_scatter(term, "mode", scatter_dimension=0, tiled=True)
    returned = lax.all_to_all(pending, "pix", 0, 0, tiled=True)
    picked = picked_of(1, returned).reshape(blocks, groups, own_rows, last)
    picked = lax.all_to_all(picked, "mode", 1, 1, tiled=True)
    last_model = jnp.concatenate(
        [
            jnp.einsum(
                "mfk,mkp->fp",
                picked[b],
                last_basis[:, :, b * block_len : (b + 1) * block_len],
                precision=PRODUCT_PRECISION,
            )
            for b in range(blocks)
        ],
        axis=1,
    )
    model_rows = model_rows + last_model
    own_means = lax.dynamic_slice_in_dim(block_means, mode_index * own_rows, own_rows, 1)
    own_centered = jnp.concatenate(
        [
            frames[:, b * block_len : (b + 1) * block_len] - own_means[b][:, None]
            for b in range(blocks)
        ],
        axis=1,
    )
    return own_centered - model_rows


def solution(mesh):
    return jax.shard_map(
        local,
        mesh=mesh,
        in_specs=(P("mode", "pix"), P("mode", "pix"), P("pix"), P()),
        out_specs=P("mode", "pix"),
        check_vma=False,
    )
```

```python
import jax
import jax.numpy as jnp
from jax import lax
from jax.sharding import PartitionSpec as P

NA = 8
K_CHUNKS = 2


HIGHEST_PRECISION = lax.Precision.HIGHEST
PRODUCT_PRECISION = lax.Precision.HIGH


def butterfly_sum(value, axes, size):
    index = lax.axis_index(axes)
    stride = 1
    while stride < size:
        radix = 4 if (size // stride) % 4 == 0 else 2
        digit = (index // stride) % radix
        arrived = [value]
        for shift in range(1, radix):
            pairs = []
            for i in range(size):
                d = (i // stride) % radix
                pairs.append((i, i + (((d + shift) % radix) - d) * stride))
            arrived.append(lax.ppermute(value, axes, pairs))
        stacked = jnp.stack(arrived, axis=0)
        total = None
        for member in range(radix):
            picked = stacked[(digit - member) % radix]
            total = picked if total is None else total + picked
        value = total
        stride *= radix
    return value


def local(frames, basis, annulus, truncation):
    own_rows, pix_dev = frames.shape
    groups = lax.axis_size("mode")
    parts = lax.axis_size("pix")
    total_frames = own_rows * groups
    blocks = annulus.shape[0]
    block_len = pix_dev // blocks
    modes_dev = basis.shape[0]
    gathered = lax.all_gather(frames, "mode", axis=0, tiled=True)
    mode_index = lax.axis_index("mode")
    onehot = (annulus[:, None] == jnp.arange(NA, dtype=jnp.int32)[None, :]).astype(jnp.float32)
    own_block_sums = jnp.stack(
        [jnp.sum(frames[:, b * block_len : (b + 1) * block_len], axis=1) for b in range(blocks)],
        axis=0,
    )
    own_sums = jnp.einsum("ba,bf->af", onehot, own_block_sums, precision=HIGHEST_PRECISION)
    frame_slot = (
        mode_index * own_rows + jnp.arange(own_rows, dtype=jnp.int32)
    )[:, None] == jnp.arange(total_frames, dtype=jnp.int32)[None, :]
    local_sums = jnp.einsum(
        "af,fg->ag", own_sums, frame_slot.astype(jnp.float32), precision=HIGHEST_PRECISION
    )
    first_group = (mode_index == 0).astype(jnp.float32)
    local_counts = jnp.sum(onehot, axis=0) * (block_len * first_group)
    own_slot = (
        lax.axis_index("pix") * blocks + jnp.arange(blocks, dtype=jnp.int32)
    )[:, None] == jnp.arange(parts * blocks, dtype=jnp.int32)[None, :]
    local_table = jnp.einsum(
        "ba,bc->ac", onehot, own_slot.astype(jnp.float32), precision=HIGHEST_PRECISION
    ) * first_group
    packed = butterfly_sum(
        jnp.concatenate([local_sums, local_counts[:, None], local_table], axis=1),
        ("pix", "mode"),
        parts * groups,
    )
    annulus_totals = packed[:, :total_frames]
    pixel_counts = packed[:, total_frames]
    every_onehot = packed[:, total_frames + 1 :].T
    mode_ids = mode_index * modes_dev + jnp.arange(modes_dev, dtype=jnp.int32)
    retained = (mode_ids[None, :] < truncation[:, None]).astype(jnp.float32)
    annulus_means = annulus_totals / pixel_counts[:, None]
    block_means = jnp.einsum("ba,af->bf", onehot, annulus_means, precision=HIGHEST_PRECISION)
    centered = [
        gathered[:, b * block_len : (b + 1) * block_len] - block_means[b][:, None]
        for b in range(blocks)
    ]
    chunk = modes_dev // K_CHUNKS
    same_annulus = jnp.einsum("ca,ba->cb", every_onehot, every_onehot, precision=HIGHEST_PRECISION)
    block_retained = jnp.einsum("ba,ak->bk", every_onehot, retained, precision=HIGHEST_PRECISION)
    rows_dev = total_frames // parts
    pieces = [
        [
            basis[c * chunk : (c + 1) * chunk, b * block_len : (b + 1) * block_len]
            for b in range(blocks)
        ]
        for c in range(K_CHUNKS)
    ]

    def outbound(c):
        return jnp.stack(
            [
                jnp.dot(centered[b], pieces[c][b].T, precision=PRODUCT_PRECISION).reshape(
                    parts, rows_dev, chunk
                )
                for b in range(blocks)
            ],
            axis=1,
        )

    def inbound(c, arrived):
        summed = jnp.einsum(
            "cb,bfk->cfk",
            same_annulus,
            arrived.reshape(parts * blocks, rows_dev, chunk),
            precision=HIGHEST_PRECISION,
        )
        outgoing = summed * block_retained[:, None, c * chunk : (c + 1) * chunk]
        return outgoing.reshape(parts, blocks, rows_dev, chunk)

    def model_of(c, returned):
        picked = returned.transpose(1, 0, 2, 3).reshape(blocks, total_frames, chunk)
        return jnp.concatenate(
            [jnp.dot(picked[b], pieces[c][b], precision=PRODUCT_PRECISION) for b in range(blocks)],
            axis=1,
        )

    term = None
    pending = None
    for stage in range(K_CHUNKS + 1):
        sending = []
        if stage < K_CHUNKS:
            sending.append(outbound(stage))
        if pending is not None:
            sending.append(pending)
        received = lax.all_to_all(jnp.stack(sending, axis=1), "pix", 0, 0, tiled=True)
        slot = 0
        next_pending = None
        if stage < K_CHUNKS:
            next_pending = inbound(stage, received[:, 0])
            slot = 1
        if pending is not None:
            part = model_of(stage - 1, received[:, slot])
            term = part if term is None else term + part
        pending = next_pending
    model_rows = lax.psum_scatter(term, "mode", scatter_dimension=0, tiled=True)
    own_means = lax.dynamic_slice_in_dim(block_means, mode_index * own_rows, own_rows, 1)
    own_centered = jnp.concatenate(
        [
            frames[:, b * block_len : (b + 1) * block_len] - own_means[b][:, None]
            for b in range(blocks)
        ],
        axis=1,
    )
    return own_centered - model_rows


def solution(mesh):
    return jax.shard_map(
        local,
        mesh=mesh,
        in_specs=(P("mode", "pix"), P("mode", "pix"), P("pix"), P()),
        out_specs=P("mode", "pix"),
        check_vma=False,
    )
```

```python
import jax
import jax.numpy as jnp
from jax import lax
from jax.sharding import PartitionSpec as P

NA = 8
K_CHUNKS = 2


HIGHEST_PRECISION = lax.Precision.HIGHEST
PRODUCT_PRECISION = lax.Precision.HIGH


def butterfly_sum(value, axes, size):
    step = 1
    while step < size:
        pairs = [(i, i ^ step) for i in range(size)]
        value = value + lax.ppermute(value, axes, pairs)
        step *= 2
    return value


def local(frames, basis, annulus, truncation):
    own_rows, pix_dev = frames.shape
    groups = lax.axis_size("mode")
    parts = lax.axis_size("pix")
    total_frames = own_rows * groups
    blocks = annulus.shape[0]
    block_len = pix_dev // blocks
    modes_dev = basis.shape[0]
    gathered = lax.all_gather(frames, "mode", axis=0, tiled=True)
    mode_index = lax.axis_index("mode")
    onehot = (annulus[:, None] == jnp.arange(NA, dtype=jnp.int32)[None, :]).astype(jnp.float32)
    own_block_sums = jnp.stack(
        [jnp.sum(frames[:, b * block_len : (b + 1) * block_len], axis=1) for b in range(blocks)],
        axis=0,
    )
    own_sums = jnp.einsum("ba,bf->af", onehot, own_block_sums, precision=HIGHEST_PRECISION)
    frame_slot = (
        mode_index * own_rows + jnp.arange(own_rows, dtype=jnp.int32)
    )[:, None] == jnp.arange(total_frames, dtype=jnp.int32)[None, :]
    local_sums = jnp.einsum(
        "af,fg->ag", own_sums, frame_slot.astype(jnp.float32), precision=HIGHEST_PRECISION
    )
    first_group = (mode_index == 0).astype(jnp.float32)
    local_counts = jnp.sum(onehot, axis=0) * (block_len * first_group)
    own_slot = (
        lax.axis_index("pix") * blocks + jnp.arange(blocks, dtype=jnp.int32)
    )[:, None] == jnp.arange(parts * blocks, dtype=jnp.int32)[None, :]
    local_table = jnp.einsum(
        "ba,bc->ac", onehot, own_slot.astype(jnp.float32), precision=HIGHEST_PRECISION
    ) * first_group
    packed = butterfly_sum(
        jnp.concatenate([local_sums, local_counts[:, None], local_table], axis=1),
        ("pix", "mode"),
        parts * groups,
    )
    annulus_totals = packed[:, :total_frames]
    pixel_counts = packed[:, total_frames]
    every_onehot = packed[:, total_frames + 1 :].T
    mode_ids = mode_index * modes_dev + jnp.arange(modes_dev, dtype=jnp.int32)
    retained = (mode_ids[None, :] < truncation[:, None]).astype(jnp.float32)
    annulus_means = annulus_totals / pixel_counts[:, None]
    block_means = jnp.einsum("ba,af->bf", onehot, annulus_means, precision=HIGHEST_PRECISION)
    centered = [
        gathered[:, b * block_len : (b + 1) * block_len] - block_means[b][:, None]
        for b in range(blocks)
    ]
    chunk = modes_dev // K_CHUNKS
    same_annulus = jnp.einsum("ca,ba->cb", every_onehot, every_onehot, precision=HIGHEST_PRECISION)
    block_retained = jnp.einsum("ba,ak->bk", every_onehot, retained, precision=HIGHEST_PRECISION)
    rows_dev = total_frames // parts
    pieces = [
        [
            basis[c * chunk : (c + 1) * chunk, b * block_len : (b + 1) * block_len]
            for b in range(blocks)
        ]
        for c in range(K_CHUNKS)
    ]

    def outbound(c):
        per_block = jnp.stack(
            [
                jnp.dot(centered[b], pieces[c][b].T, precision=PRODUCT_PRECISION)
                for b in range(blocks)
            ],
            axis=0,
        )
        return per_block.reshape(blocks, parts, rows_dev, chunk).transpose(1, 0, 2, 3)

    def inbound(c, arrived):
        summed = jnp.einsum(
            "cb,bfk->cfk",
            same_annulus,
            arrived.reshape(parts * blocks, rows_dev, chunk),
            precision=HIGHEST_PRECISION,
        )
        outgoing = summed * block_retained[:, None, c * chunk : (c + 1) * chunk]
        return outgoing.reshape(parts, blocks, rows_dev, chunk)

    whole_basis = lax.all_gather(basis, "mode", axis=0, tiled=True).reshape(
        groups, modes_dev, pix_dev
    )

    def model_of(c, returned):
        picked = returned.transpose(1, 0, 2, 3).reshape(blocks, groups, own_rows, chunk)
        picked = lax.all_to_all(picked, "mode", 1, 1, tiled=True)
        return jnp.concatenate(
            [
                jnp.einsum(
                    "mfk,mkp->fp",
                    picked[b],
                    whole_basis[:, c * chunk : (c + 1) * chunk, b * block_len : (b + 1) * block_len],
                    precision=PRODUCT_PRECISION,
                )
                for b in range(blocks)
            ],
            axis=1,
        )

    term = None
    pending = None
    for stage in range(K_CHUNKS + 1):
        sending = []
        if stage < K_CHUNKS:
            sending.append(outbound(stage))
        if pending is not None:
            sending.append(pending)
        received = lax.all_to_all(jnp.stack(sending, axis=1), "pix", 0, 0, tiled=True)
        slot = 0
        next_pending = None
        if stage < K_CHUNKS:
            next_pending = inbound(stage, received[:, 0])
            slot = 1
        if pending is not None:
            part = model_of(stage - 1, received[:, slot])
            term = part if term is None else term + part
        pending = next_pending
    model_rows = term
    own_means = lax.dynamic_slice_in_dim(block_means, mode_index * own_rows, own_rows, 1)
    own_centered = jnp.concatenate(
        [
            frames[:, b * block_len : (b + 1) * block_len] - own_means[b][:, None]
            for b in range(blocks)
        ],
        axis=1,
    )
    return own_centered - model_rows


def solution(mesh):
    return jax.shard_map(
        local,
        mesh=mesh,
        in_specs=(P("mode", "pix"), P("mode", "pix"), P("pix"), P()),
        out_specs=P("mode", "pix"),
        check_vma=False,
    )
```

```python
import jax
import jax.numpy as jnp
from jax import lax
from jax.sharding import PartitionSpec as P

NA = 8
K_CHUNKS = 2


HIGHEST_PRECISION = lax.Precision.HIGHEST
PRODUCT_PRECISION = lax.Precision.HIGH


def butterfly_sum(value, axes, size):
    step = 1
    while step < size:
        pairs = [(i, i ^ step) for i in range(size)]
        value = value + lax.ppermute(value, axes, pairs)
        step *= 2
    return value


def local(frames, basis, annulus, truncation):
    own_rows, pix_dev = frames.shape
    groups = lax.axis_size("mode")
    parts = lax.axis_size("pix")
    total_frames = own_rows * groups
    blocks = annulus.shape[0]
    block_len = pix_dev // blocks
    modes_dev = basis.shape[0]
    gathered = lax.all_gather(frames, "mode", axis=0, tiled=True)
    mode_index = lax.axis_index("mode")
    onehot = (annulus[:, None] == jnp.arange(NA, dtype=jnp.int32)[None, :]).astype(jnp.float32)
    own_block_sums = jnp.stack(
        [jnp.sum(frames[:, b * block_len : (b + 1) * block_len], axis=1) for b in range(blocks)],
        axis=0,
    )
    own_sums = jnp.einsum("ba,bf->af", onehot, own_block_sums, precision=HIGHEST_PRECISION)
    frame_slot = (
        mode_index * own_rows + jnp.arange(own_rows, dtype=jnp.int32)
    )[:, None] == jnp.arange(total_frames, dtype=jnp.int32)[None, :]
    local_sums = jnp.einsum(
        "af,fg->ag", own_sums, frame_slot.astype(jnp.float32), precision=HIGHEST_PRECISION
    )
    first_group = (mode_index == 0).astype(jnp.float32)
    local_counts = jnp.sum(onehot, axis=0) * (block_len * first_group)
    own_slot = (
        lax.axis_index("pix") * blocks + jnp.arange(blocks, dtype=jnp.int32)
    )[:, None] == jnp.arange(parts * blocks, dtype=jnp.int32)[None, :]
    local_table = jnp.einsum(
        "ba,bc->ac", onehot, own_slot.astype(jnp.float32), precision=HIGHEST_PRECISION
    ) * first_group
    packed = butterfly_sum(
        jnp.concatenate([local_sums, local_counts[:, None], local_table], axis=1),
        ("pix", "mode"),
        parts * groups,
    )
    annulus_totals = packed[:, :total_frames]
    pixel_counts = packed[:, total_frames]
    every_onehot = packed[:, total_frames + 1 :].T
    mode_ids = mode_index * modes_dev + jnp.arange(modes_dev, dtype=jnp.int32)
    retained = (mode_ids[None, :] < truncation[:, None]).astype(jnp.float32)
    annulus_means = annulus_totals / pixel_counts[:, None]
    block_means = jnp.einsum("ba,af->bf", onehot, annulus_means, precision=HIGHEST_PRECISION)
    centered = [
        gathered[:, b * block_len : (b + 1) * block_len] - block_means[b][:, None]
        for b in range(blocks)
    ]
    chunk = modes_dev // K_CHUNKS
    same_annulus = jnp.einsum("ca,ba->cb", every_onehot, every_onehot, precision=HIGHEST_PRECISION)
    block_retained = jnp.einsum("ba,ak->bk", every_onehot, retained, precision=HIGHEST_PRECISION)
    rows_dev = total_frames // parts
    pieces = [
        [
            basis[c * chunk : (c + 1) * chunk, b * block_len : (b + 1) * block_len]
            for b in range(blocks)
        ]
        for c in range(K_CHUNKS)
    ]

    def outbound(c):
        per_block = jnp.stack(
            [
                jnp.dot(centered[b], pieces[c][b].T, precision=PRODUCT_PRECISION)
                for b in range(blocks)
            ],
            axis=0,
        )
        return per_block.reshape(blocks, parts, rows_dev, chunk).transpose(1, 0, 2, 3)

    def inbound(c, arrived):
        summed = jnp.einsum(
            "cb,bfk->cfk",
            same_annulus,
            arrived.reshape(parts * blocks, rows_dev, chunk),
            precision=HIGHEST_PRECISION,
        )
        outgoing = summed * block_retained[:, None, c * chunk : (c + 1) * chunk]
        return outgoing.reshape(parts, blocks, rows_dev, chunk)

    whole_basis = lax.all_gather(basis, "mode", axis=0, tiled=True).reshape(
        groups, modes_dev, pix_dev
    )

    def model_of(c, returned):
        picked = returned.transpose(1, 0, 2, 3).reshape(blocks, groups, own_rows, chunk)
        if c == K_CHUNKS - 1:
            picked = lax.all_to_all(picked, "mode", 1, 1, tiled=True)
        else:
            from_each = [lax.dynamic_index_in_dim(picked, mode_index, 1, keepdims=False)]
            for shift in range(1, groups):
                target = (mode_index + shift) % groups
                sent = lax.dynamic_index_in_dim(picked, target, 1, keepdims=False)
                pairs = [(m, (m + shift) % groups) for m in range(groups)]
                from_each.append(lax.ppermute(sent, "mode", pairs))
            stacked = jnp.stack(from_each, axis=1)
            order = (mode_index - jnp.arange(groups, dtype=jnp.int32)) % groups
            picked = jnp.take(stacked, order, axis=1)
        return jnp.concatenate(
            [
                jnp.einsum(
                    "mfk,mkp->fp",
                    picked[b],
                    whole_basis[:, c * chunk : (c + 1) * chunk, b * block_len : (b + 1) * block_len],
                    precision=PRODUCT_PRECISION,
                )
                for b in range(blocks)
            ],
            axis=1,
        )

    term = None
    pending = None
    for stage in range(K_CHUNKS + 1):
        sending = []
        if stage < K_CHUNKS:
            sending.append(outbound(stage))
        if pending is not None:
            sending.append(pending)
        received = lax.all_to_all(jnp.stack(sending, axis=1), "pix", 0, 0, tiled=True)
        slot = 0
        next_pending = None
        if stage < K_CHUNKS:
            next_pending = inbound(stage, received[:, 0])
            slot = 1
        if pending is not None:
            part = model_of(stage - 1, received[:, slot])
            term = part if term is None else term + part
        pending = next_pending
    model_rows = term
    own_means = lax.dynamic_slice_in_dim(block_means, mode_index * own_rows, own_rows, 1)
    own_centered = jnp.concatenate(
        [
            frames[:, b * block_len : (b + 1) * block_len] - own_means[b][:, None]
            for b in range(blocks)
        ],
        axis=1,
    )
    return own_centered - model_rows


def solution(mesh):
    return jax.shard_map(
        local,
        mesh=mesh,
        in_specs=(P("mode", "pix"), P("mode", "pix"), P("pix"), P()),
        out_specs=P("mode", "pix"),
        check_vma=False,
    )
```

```python
import jax
import jax.numpy as jnp
from jax import lax
from jax.sharding import PartitionSpec as P

NA = 8
K_CHUNKS = 2


HIGHEST_PRECISION = lax.Precision.HIGHEST
PRODUCT_PRECISION = lax.Precision.HIGH


def butterfly_sum(value, axes, size):
    step = 1
    while step < size:
        pairs = [(i, i ^ step) for i in range(size)]
        value = value + lax.ppermute(value, axes, pairs)
        step *= 2
    return value


def local(frames, basis, annulus, truncation):
    own_rows, pix_dev = frames.shape
    groups = lax.axis_size("mode")
    parts = lax.axis_size("pix")
    total_frames = own_rows * groups
    blocks = annulus.shape[0]
    block_len = pix_dev // blocks
    modes_dev = basis.shape[0]
    gathered = lax.all_gather(frames, "mode", axis=0, tiled=True)
    mode_index = lax.axis_index("mode")
    onehot = (annulus[:, None] == jnp.arange(NA, dtype=jnp.int32)[None, :]).astype(jnp.float32)
    own_block_sums = jnp.stack(
        [jnp.sum(frames[:, b * block_len : (b + 1) * block_len], axis=1) for b in range(blocks)],
        axis=0,
    )
    own_sums = jnp.einsum("ba,bf->af", onehot, own_block_sums, precision=HIGHEST_PRECISION)
    frame_slot = (
        mode_index * own_rows + jnp.arange(own_rows, dtype=jnp.int32)
    )[:, None] == jnp.arange(total_frames, dtype=jnp.int32)[None, :]
    local_sums = jnp.einsum(
        "af,fg->ag", own_sums, frame_slot.astype(jnp.float32), precision=HIGHEST_PRECISION
    )
    first_group = (mode_index == 0).astype(jnp.float32)
    local_counts = jnp.sum(onehot, axis=0) * (block_len * first_group)
    own_slot = (
        lax.axis_index("pix") * blocks + jnp.arange(blocks, dtype=jnp.int32)
    )[:, None] == jnp.arange(parts * blocks, dtype=jnp.int32)[None, :]
    local_table = jnp.einsum(
        "ba,bc->ac", onehot, own_slot.astype(jnp.float32), precision=HIGHEST_PRECISION
    ) * first_group
    packed = butterfly_sum(
        jnp.concatenate([local_sums, local_counts[:, None], local_table], axis=1),
        ("pix", "mode"),
        parts * groups,
    )
    annulus_totals = packed[:, :total_frames]
    pixel_counts = packed[:, total_frames]
    every_onehot = packed[:, total_frames + 1 :].T
    mode_ids = mode_index * modes_dev + jnp.arange(modes_dev, dtype=jnp.int32)
    retained = (mode_ids[None, :] < truncation[:, None]).astype(jnp.float32)
    annulus_means = annulus_totals / pixel_counts[:, None]
    block_means = jnp.einsum("ba,af->bf", onehot, annulus_means, precision=HIGHEST_PRECISION)
    chunk = modes_dev // K_CHUNKS
    same_annulus = jnp.einsum("ca,ba->cb", every_onehot, every_onehot, precision=HIGHEST_PRECISION)
    block_retained = jnp.einsum("ba,ak->bk", every_onehot, retained, precision=HIGHEST_PRECISION)
    rows_dev = total_frames // parts

    def piece_of(c, b):
        return lax.dynamic_slice(basis, (c * chunk, b * block_len), (chunk, block_len))

    def outbound(c):
        def body(b, per_block):
            mean = lax.dynamic_index_in_dim(block_means, b, 0, keepdims=False)
            centered = lax.dynamic_slice_in_dim(gathered, b * block_len, block_len, 1) - mean[:, None]
            product = jnp.dot(centered, piece_of(c, b).T, precision=PRODUCT_PRECISION)
            return lax.dynamic_update_index_in_dim(per_block, product, b, 0)

        per_block = lax.fori_loop(
            0, blocks, body, jnp.zeros((blocks, total_frames, chunk), jnp.float32)
        )
        return per_block.reshape(blocks, parts, rows_dev, chunk).transpose(1, 0, 2, 3)

    def inbound(c, arrived):
        summed = jnp.einsum(
            "cb,bfk->cfk",
            same_annulus,
            arrived.reshape(parts * blocks, rows_dev, chunk),
            precision=HIGHEST_PRECISION,
        )
        outgoing = summed * block_retained[:, None, c * chunk : (c + 1) * chunk]
        return outgoing.reshape(parts, blocks, rows_dev, chunk)

    def model_of(c, returned):
        picked = returned.transpose(1, 0, 2, 3).reshape(blocks, total_frames, chunk)

        def body(b, term):
            coefficients = lax.dynamic_index_in_dim(picked, b, 0, keepdims=False)
            product = jnp.dot(coefficients, piece_of(c, b), precision=PRODUCT_PRECISION)
            return lax.dynamic_update_slice_in_dim(term, product, b * block_len, 1)

        return lax.fori_loop(0, blocks, body, jnp.zeros((total_frames, pix_dev), jnp.float32))

    term = None
    pending = None
    for stage in range(K_CHUNKS + 1):
        sending = []
        if stage < K_CHUNKS:
            sending.append(outbound(stage))
        if pending is not None:
            sending.append(pending)
        received = lax.all_to_all(jnp.stack(sending, axis=1), "pix", 0, 0, tiled=True)
        slot = 0
        next_pending = None
        if stage < K_CHUNKS:
            next_pending = inbound(stage, received[:, 0])
            slot = 1
        if pending is not None:
            part = model_of(stage - 1, received[:, slot])
            term = part if term is None else term + part
        pending = next_pending
    model_rows = lax.psum_scatter(term, "mode", scatter_dimension=0, tiled=True)
    own_means = lax.dynamic_slice_in_dim(block_means, mode_index * own_rows, own_rows, 1)
    own_centered = jnp.concatenate(
        [
            frames[:, b * block_len : (b + 1) * block_len] - own_means[b][:, None]
            for b in range(blocks)
        ],
        axis=1,
    )
    return own_centered - model_rows


def solution(mesh):
    return jax.shard_map(
        local,
        mesh=mesh,
        in_specs=(P("mode", "pix"), P("mode", "pix"), P("pix"), P()),
        out_specs=P("mode", "pix"),
        check_vma=False,
    )
```

```python
import jax
import jax.numpy as jnp
from jax import lax
from jax.sharding import PartitionSpec as P

NA = 8
K_CHUNKS = 2


HIGHEST_PRECISION = lax.Precision.HIGHEST
PRODUCT_PRECISION = lax.Precision.HIGH


def butterfly_sum(value, axes, size):
    step = 1
    while step < size:
        pairs = [(i, i ^ step) for i in range(size)]
        value = value + lax.ppermute(value, axes, pairs)
        step *= 2
    return value


def local(frames, basis, annulus, truncation):
    own_rows, pix_dev = frames.shape
    groups = lax.axis_size("mode")
    parts = lax.axis_size("pix")
    total_frames = own_rows * groups
    blocks = annulus.shape[0]
    block_len = pix_dev // blocks
    modes_dev = basis.shape[0]
    gathered = lax.all_gather(frames, "mode", axis=0, tiled=True)
    mode_index = lax.axis_index("mode")
    onehot = (annulus[:, None] == jnp.arange(NA, dtype=jnp.int32)[None, :]).astype(jnp.float32)
    own_block_sums = jnp.stack(
        [jnp.sum(frames[:, b * block_len : (b + 1) * block_len], axis=1) for b in range(blocks)],
        axis=0,
    )
    own_sums = jnp.einsum("ba,bf->af", onehot, own_block_sums, precision=HIGHEST_PRECISION)
    frame_slot = (
        mode_index * own_rows + jnp.arange(own_rows, dtype=jnp.int32)
    )[:, None] == jnp.arange(total_frames, dtype=jnp.int32)[None, :]
    local_sums = jnp.einsum(
        "af,fg->ag", own_sums, frame_slot.astype(jnp.float32), precision=HIGHEST_PRECISION
    )
    first_group = (mode_index == 0).astype(jnp.float32)
    local_counts = jnp.sum(onehot, axis=0) * (block_len * first_group)
    own_slot = (
        lax.axis_index("pix") * blocks + jnp.arange(blocks, dtype=jnp.int32)
    )[:, None] == jnp.arange(parts * blocks, dtype=jnp.int32)[None, :]
    local_table = jnp.einsum(
        "ba,bc->ac", onehot, own_slot.astype(jnp.float32), precision=HIGHEST_PRECISION
    ) * first_group
    packed = butterfly_sum(
        jnp.concatenate([local_sums, local_counts[:, None], local_table], axis=1),
        ("pix", "mode"),
        parts * groups,
    )
    annulus_totals = packed[:, :total_frames]
    pixel_counts = packed[:, total_frames]
    every_onehot = packed[:, total_frames + 1 :].T
    mode_ids = mode_index * modes_dev + jnp.arange(modes_dev, dtype=jnp.int32)
    retained = (mode_ids[None, :] < truncation[:, None]).astype(jnp.float32)
    annulus_means = annulus_totals / pixel_counts[:, None]
    block_means = jnp.einsum("ba,af->bf", onehot, annulus_means, precision=HIGHEST_PRECISION)
    centered = [
        gathered[:, b * block_len : (b + 1) * block_len] - block_means[b][:, None]
        for b in range(blocks)
    ]
    chunk = modes_dev // K_CHUNKS
    same_annulus = jnp.einsum("ca,ba->cb", every_onehot, every_onehot, precision=HIGHEST_PRECISION)
    block_retained = jnp.einsum("ba,ak->bk", every_onehot, retained, precision=HIGHEST_PRECISION)
    rows_dev = total_frames // parts
    pieces = [
        [
            basis[c * chunk : (c + 1) * chunk, b * block_len : (b + 1) * block_len]
            for b in range(blocks)
        ]
        for c in range(K_CHUNKS)
    ]

    def outbound(c):
        per_block = jnp.stack(
            [
                jnp.dot(centered[b], pieces[c][b].T, precision=PRODUCT_PRECISION)
                for b in range(blocks)
            ],
            axis=0,
        )
        return per_block.reshape(blocks, parts, rows_dev, chunk).transpose(1, 0, 2, 3)

    def inbound(c, arrived):
        summed = jnp.einsum(
            "cb,bfk->cfk",
            same_annulus,
            arrived.reshape(parts * blocks, rows_dev, chunk),
            precision=HIGHEST_PRECISION,
        )
        outgoing = summed * block_retained[:, None, c * chunk : (c + 1) * chunk]
        return outgoing.reshape(parts, blocks, rows_dev, chunk)

    def model_of(c, returned):
        picked = returned.transpose(1, 0, 2, 3).reshape(blocks, total_frames, chunk)
        return jnp.concatenate(
            [jnp.dot(picked[b], pieces[c][b], precision=PRODUCT_PRECISION) for b in range(blocks)],
            axis=1,
        )

    term = None
    pending = None
    for stage in range(K_CHUNKS + 1):
        sending = []
        if stage < K_CHUNKS:
            sending.append(outbound(stage))
        if pending is not None:
            sending.append(pending)
        received = lax.all_to_all(jnp.stack(sending, axis=1), "pix", 0, 0, tiled=True)
        slot = 0
        next_pending = None
        if stage < K_CHUNKS:
            next_pending = inbound(stage, received[:, 0])
            slot = 1
        if pending is not None:
            part = model_of(stage - 1, received[:, slot])
            term = part if term is None else term + part
        pending = next_pending
    shares = lax.all_to_all(term.reshape(groups, own_rows, pix_dev), "mode", 0, 0, tiled=True)
    model_rows = shares[0]
    for g in range(1, groups):
        model_rows = model_rows + shares[g]
    own_means = lax.dynamic_slice_in_dim(block_means, mode_index * own_rows, own_rows, 1)
    own_centered = jnp.concatenate(
        [
            frames[:, b * block_len : (b + 1) * block_len] - own_means[b][:, None]
            for b in range(blocks)
        ],
        axis=1,
    )
    return own_centered - model_rows


def solution(mesh):
    return jax.shard_map(
        local,
        mesh=mesh,
        in_specs=(P("mode", "pix"), P("mode", "pix"), P("pix"), P()),
        out_specs=P("mode", "pix"),
        check_vma=False,
    )
```

```python
import jax
import jax.numpy as jnp
from jax import lax
from jax.sharding import PartitionSpec as P

NA = 8
K_CHUNKS = 2


HIGHEST_PRECISION = lax.Precision.HIGHEST
PRODUCT_PRECISION = lax.Precision.HIGH


def butterfly_sum(value, axes, size):
    step = 1
    while step < size:
        pairs = [(i, i ^ step) for i in range(size)]
        value = value + lax.ppermute(value, axes, pairs)
        step *= 2
    return value


def local(frames, basis, annulus, truncation):
    own_rows, pix_dev = frames.shape
    groups = lax.axis_size("mode")
    parts = lax.axis_size("pix")
    total_frames = own_rows * groups
    blocks = annulus.shape[0]
    block_len = pix_dev // blocks
    modes_dev = basis.shape[0]
    gathered = lax.all_to_all(
        jnp.broadcast_to(frames[None], (groups, own_rows, pix_dev)), "mode", 0, 0, tiled=True
    ).reshape(total_frames, pix_dev)
    mode_index = lax.axis_index("mode")
    onehot = (annulus[:, None] == jnp.arange(NA, dtype=jnp.int32)[None, :]).astype(jnp.float32)
    own_block_sums = jnp.stack(
        [jnp.sum(frames[:, b * block_len : (b + 1) * block_len], axis=1) for b in range(blocks)],
        axis=0,
    )
    own_sums = jnp.einsum("ba,bf->af", onehot, own_block_sums, precision=HIGHEST_PRECISION)
    frame_slot = (
        mode_index * own_rows + jnp.arange(own_rows, dtype=jnp.int32)
    )[:, None] == jnp.arange(total_frames, dtype=jnp.int32)[None, :]
    local_sums = jnp.einsum(
        "af,fg->ag", own_sums, frame_slot.astype(jnp.float32), precision=HIGHEST_PRECISION
    )
    first_group = (mode_index == 0).astype(jnp.float32)
    local_counts = jnp.sum(onehot, axis=0) * (block_len * first_group)
    own_slot = (
        lax.axis_index("pix") * blocks + jnp.arange(blocks, dtype=jnp.int32)
    )[:, None] == jnp.arange(parts * blocks, dtype=jnp.int32)[None, :]
    local_table = jnp.einsum(
        "ba,bc->ac", onehot, own_slot.astype(jnp.float32), precision=HIGHEST_PRECISION
    ) * first_group
    packed = butterfly_sum(
        jnp.concatenate([local_sums, local_counts[:, None], local_table], axis=1),
        ("pix", "mode"),
        parts * groups,
    )
    annulus_totals = packed[:, :total_frames]
    pixel_counts = packed[:, total_frames]
    every_onehot = packed[:, total_frames + 1 :].T
    mode_ids = mode_index * modes_dev + jnp.arange(modes_dev, dtype=jnp.int32)
    retained = (mode_ids[None, :] < truncation[:, None]).astype(jnp.float32)
    annulus_means = annulus_totals / pixel_counts[:, None]
    block_means = jnp.einsum("ba,af->bf", onehot, annulus_means, precision=HIGHEST_PRECISION)
    centered = [
        gathered[:, b * block_len : (b + 1) * block_len] - block_means[b][:, None]
        for b in range(blocks)
    ]
    chunk = modes_dev // K_CHUNKS
    same_annulus = jnp.einsum("ca,ba->cb", every_onehot, every_onehot, precision=HIGHEST_PRECISION)
    block_retained = jnp.einsum("ba,ak->bk", every_onehot, retained, precision=HIGHEST_PRECISION)
    rows_dev = total_frames // parts
    pieces = [
        [
            basis[c * chunk : (c + 1) * chunk, b * block_len : (b + 1) * block_len]
            for b in range(blocks)
        ]
        for c in range(K_CHUNKS)
    ]

    def outbound(c):
        per_block = jnp.stack(
            [
                jnp.dot(centered[b], pieces[c][b].T, precision=PRODUCT_PRECISION)
                for b in range(blocks)
            ],
            axis=0,
        )
        return per_block.reshape(blocks, parts, rows_dev, chunk).transpose(1, 0, 2, 3)

    def inbound(c, arrived):
        summed = jnp.einsum(
            "cb,bfk->cfk",
            same_annulus,
            arrived.reshape(parts * blocks, rows_dev, chunk),
            precision=HIGHEST_PRECISION,
        )
        outgoing = summed * block_retained[:, None, c * chunk : (c + 1) * chunk]
        return outgoing.reshape(parts, blocks, rows_dev, chunk)

    def model_of(c, returned):
        picked = returned.transpose(1, 0, 2, 3).reshape(blocks, total_frames, chunk)
        return jnp.concatenate(
            [jnp.dot(picked[b], pieces[c][b], precision=PRODUCT_PRECISION) for b in range(blocks)],
            axis=1,
        )

    term = None
    pending = None
    for stage in range(K_CHUNKS + 1):
        sending = []
        if stage < K_CHUNKS:
            sending.append(outbound(stage))
        if pending is not None:
            sending.append(pending)
        received = lax.all_to_all(jnp.stack(sending, axis=1), "pix", 0, 0, tiled=True)
        slot = 0
        next_pending = None
        if stage < K_CHUNKS:
            next_pending = inbound(stage, received[:, 0])
            slot = 1
        if pending is not None:
            part = model_of(stage - 1, received[:, slot])
            term = part if term is None else term + part
        pending = next_pending
    shares = lax.all_to_all(term.reshape(groups, own_rows, pix_dev), "mode", 0, 0, tiled=True)
    model_rows = shares[0]
    for g in range(1, groups):
        model_rows = model_rows + shares[g]
    own_means = lax.dynamic_slice_in_dim(block_means, mode_index * own_rows, own_rows, 1)
    own_centered = jnp.concatenate(
        [
            frames[:, b * block_len : (b + 1) * block_len] - own_means[b][:, None]
            for b in range(blocks)
        ],
        axis=1,
    )
    return own_centered - model_rows


def solution(mesh):
    return jax.shard_map(
        local,
        mesh=mesh,
        in_specs=(P("mode", "pix"), P("mode", "pix"), P("pix"), P()),
        out_specs=P("mode", "pix"),
        check_vma=False,
    )
```

```python
import jax
import jax.numpy as jnp
from jax import lax
from jax.sharding import PartitionSpec as P

NA = 8
K_CHUNKS = 4


HIGHEST_PRECISION = lax.Precision.HIGHEST
PRODUCT_PRECISION = lax.Precision.HIGH


def butterfly_sum(value, axes, size):
    step = 1
    while step < size:
        pairs = [(i, i ^ step) for i in range(size)]
        value = value + lax.ppermute(value, axes, pairs)
        step *= 2
    return value


def local(frames, basis, annulus, truncation):
    own_rows, pix_dev = frames.shape
    groups = lax.axis_size("mode")
    parts = lax.axis_size("pix")
    total_frames = own_rows * groups
    blocks = annulus.shape[0]
    block_len = pix_dev // blocks
    modes_dev = basis.shape[0]
    gathered = lax.all_gather(frames, "mode", axis=0, tiled=True)
    mode_index = lax.axis_index("mode")
    onehot = (annulus[:, None] == jnp.arange(NA, dtype=jnp.int32)[None, :]).astype(jnp.float32)
    own_block_sums = jnp.stack(
        [jnp.sum(frames[:, b * block_len : (b + 1) * block_len], axis=1) for b in range(blocks)],
        axis=0,
    )
    own_sums = jnp.einsum("ba,bf->af", onehot, own_block_sums, precision=HIGHEST_PRECISION)
    frame_slot = (
        mode_index * own_rows + jnp.arange(own_rows, dtype=jnp.int32)
    )[:, None] == jnp.arange(total_frames, dtype=jnp.int32)[None, :]
    local_sums = jnp.einsum(
        "af,fg->ag", own_sums, frame_slot.astype(jnp.float32), precision=HIGHEST_PRECISION
    )
    first_group = (mode_index == 0).astype(jnp.float32)
    local_counts = jnp.sum(onehot, axis=0) * (block_len * first_group)
    own_slot = (
        lax.axis_index("pix") * blocks + jnp.arange(blocks, dtype=jnp.int32)
    )[:, None] == jnp.arange(parts * blocks, dtype=jnp.int32)[None, :]
    local_table = jnp.einsum(
        "ba,bc->ac", onehot, own_slot.astype(jnp.float32), precision=HIGHEST_PRECISION
    ) * first_group
    packed = butterfly_sum(
        jnp.concatenate([local_sums, local_counts[:, None], local_table], axis=1),
        ("pix", "mode"),
        parts * groups,
    )
    annulus_totals = packed[:, :total_frames]
    pixel_counts = packed[:, total_frames]
    every_onehot = packed[:, total_frames + 1 :].T
    mode_ids = mode_index * modes_dev + jnp.arange(modes_dev, dtype=jnp.int32)
    retained = (mode_ids[None, :] < truncation[:, None]).astype(jnp.float32)
    annulus_means = annulus_totals / pixel_counts[:, None]
    block_means = jnp.einsum("ba,af->bf", onehot, annulus_means, precision=HIGHEST_PRECISION)
    centered = [
        gathered[:, b * block_len : (b + 1) * block_len] - block_means[b][:, None]
        for b in range(blocks)
    ]
    chunk = modes_dev // K_CHUNKS
    same_annulus = jnp.einsum("ca,ba->cb", every_onehot, every_onehot, precision=HIGHEST_PRECISION)
    block_retained = jnp.einsum("ba,ak->bk", every_onehot, retained, precision=HIGHEST_PRECISION)
    rows_dev = total_frames // parts
    pieces = [
        [
            basis[c * chunk : (c + 1) * chunk, b * block_len : (b + 1) * block_len]
            for b in range(blocks)
        ]
        for c in range(K_CHUNKS)
    ]

    def outbound(c):
        per_block = jnp.stack(
            [
                jnp.dot(centered[b], pieces[c][b].T, precision=PRODUCT_PRECISION)
                for b in range(blocks)
            ],
            axis=0,
        )
        return per_block.reshape(blocks, parts, rows_dev, chunk).transpose(1, 0, 2, 3)

    def inbound(c, arrived):
        summed = jnp.einsum(
            "cb,bfk->cfk",
            same_annulus,
            arrived.reshape(parts * blocks, rows_dev, chunk),
            precision=HIGHEST_PRECISION,
        )
        outgoing = summed * block_retained[:, None, c * chunk : (c + 1) * chunk]
        return outgoing.reshape(parts, blocks, rows_dev, chunk)

    def model_of(c, returned):
        picked = returned.transpose(1, 0, 2, 3).reshape(blocks, total_frames, chunk)
        return jnp.concatenate(
            [jnp.dot(picked[b], pieces[c][b], precision=PRODUCT_PRECISION) for b in range(blocks)],
            axis=1,
        )

    term = None
    pending = None
    for stage in range(K_CHUNKS + 1):
        sending = []
        if stage < K_CHUNKS:
            sending.append(outbound(stage))
        if pending is not None:
            sending.append(pending)
        received = lax.all_to_all(jnp.stack(sending, axis=1), "pix", 0, 0, tiled=True)
        slot = 0
        next_pending = None
        if stage < K_CHUNKS:
            next_pending = inbound(stage, received[:, 0])
            slot = 1
        if pending is not None:
            part = model_of(stage - 1, received[:, slot])
            term = part if term is None else term + part
        pending = next_pending
    model_rows = lax.psum_scatter(term, "mode", scatter_dimension=0, tiled=True)
    own_means = lax.dynamic_slice_in_dim(block_means, mode_index * own_rows, own_rows, 1)
    own_centered = jnp.concatenate(
        [
            frames[:, b * block_len : (b + 1) * block_len] - own_means[b][:, None]
            for b in range(blocks)
        ],
        axis=1,
    )
    return own_centered - model_rows


def solution(mesh):
    return jax.shard_map(
        local,
        mesh=mesh,
        in_specs=(P("mode", "pix"), P("mode", "pix"), P("pix"), P()),
        out_specs=P("mode", "pix"),
        check_vma=False,
    )
```

```python
import jax
import jax.numpy as jnp
from jax import lax
from jax.sharding import PartitionSpec as P

NA = 8
K_CHUNKS = 2


HIGHEST_PRECISION = lax.Precision.HIGHEST
PRODUCT_PRECISION = lax.Precision.HIGH


def butterfly_sum(value, axes, size):
    step = 1
    while step < size:
        pairs = [(i, i ^ step) for i in range(size)]
        value = value + lax.ppermute(value, axes, pairs)
        step *= 2
    return value


def local(frames, basis, annulus, truncation):
    own_rows, pix_dev = frames.shape
    groups = lax.axis_size("mode")
    parts = lax.axis_size("pix")
    total_frames = own_rows * groups
    blocks = annulus.shape[0]
    block_len = pix_dev // blocks
    modes_dev = basis.shape[0]
    gathered = lax.all_gather(frames, "mode", axis=0, tiled=True)
    mode_index = lax.axis_index("mode")
    onehot = (annulus[:, None] == jnp.arange(NA, dtype=jnp.int32)[None, :]).astype(jnp.float32)
    own_block_sums = jnp.stack(
        [jnp.sum(frames[:, b * block_len : (b + 1) * block_len], axis=1) for b in range(blocks)],
        axis=0,
    )
    own_sums = jnp.einsum("ba,bf->af", onehot, own_block_sums, precision=HIGHEST_PRECISION)
    frame_slot = (
        mode_index * own_rows + jnp.arange(own_rows, dtype=jnp.int32)
    )[:, None] == jnp.arange(total_frames, dtype=jnp.int32)[None, :]
    local_sums = jnp.einsum(
        "af,fg->ag", own_sums, frame_slot.astype(jnp.float32), precision=HIGHEST_PRECISION
    )
    first_group = (mode_index == 0).astype(jnp.float32)
    local_counts = jnp.sum(onehot, axis=0) * (block_len * first_group)
    own_slot = (
        lax.axis_index("pix") * blocks + jnp.arange(blocks, dtype=jnp.int32)
    )[:, None] == jnp.arange(parts * blocks, dtype=jnp.int32)[None, :]
    local_table = jnp.einsum(
        "ba,bc->ac", onehot, own_slot.astype(jnp.float32), precision=HIGHEST_PRECISION
    ) * first_group
    packed = butterfly_sum(
        jnp.concatenate([local_sums, local_counts[:, None], local_table], axis=1),
        ("pix", "mode"),
        parts * groups,
    )
    annulus_totals = packed[:, :total_frames]
    pixel_counts = packed[:, total_frames]
    every_onehot = packed[:, total_frames + 1 :].T
    mode_ids = mode_index * modes_dev + jnp.arange(modes_dev, dtype=jnp.int32)
    retained = (mode_ids[None, :] < truncation[:, None]).astype(jnp.float32)
    annulus_means = annulus_totals / pixel_counts[:, None]
    block_means = jnp.einsum("ba,af->bf", onehot, annulus_means, precision=HIGHEST_PRECISION)
    centered = [
        gathered[:, b * block_len : (b + 1) * block_len] - block_means[b][:, None]
        for b in range(blocks)
    ]
    same_annulus = jnp.einsum("ca,ba->cb", every_onehot, every_onehot, precision=HIGHEST_PRECISION)
    block_retained = jnp.einsum("ba,ak->bk", every_onehot, retained, precision=HIGHEST_PRECISION)
    rows_dev = total_frames // parts
    split = (modes_dev * 5 // 8) // 128 * 128 or modes_dev // 2
    bounds = [(0, split), (split, modes_dev)]
    pieces = [
        [basis[lo:hi, b * block_len : (b + 1) * block_len] for b in range(blocks)]
        for lo, hi in bounds
    ]

    def outbound(c):
        width = bounds[c][1] - bounds[c][0]
        per_block = jnp.stack(
            [
                jnp.dot(centered[b], pieces[c][b].T, precision=PRODUCT_PRECISION)
                for b in range(blocks)
            ],
            axis=0,
        )
        return per_block.reshape(blocks, parts, rows_dev, width).transpose(1, 0, 2, 3)

    def inbound(c, arrived):
        lo, hi = bounds[c]
        summed = jnp.einsum(
            "cb,bfk->cfk",
            same_annulus,
            arrived.reshape(parts * blocks, rows_dev, hi - lo),
            precision=HIGHEST_PRECISION,
        )
        outgoing = summed * block_retained[:, None, lo:hi]
        return outgoing.reshape(parts, blocks, rows_dev, hi - lo)

    def model_of(c, returned):
        width = bounds[c][1] - bounds[c][0]
        picked = returned.transpose(1, 0, 2, 3).reshape(blocks, total_frames, width)
        return jnp.concatenate(
            [jnp.dot(picked[b], pieces[c][b], precision=PRODUCT_PRECISION) for b in range(blocks)],
            axis=1,
        )

    arrived = lax.all_to_all(outbound(0), "pix", 0, 0, tiled=True)
    pending = inbound(0, arrived)
    second_out = outbound(1)
    width_one = bounds[1][1] - bounds[1][0]
    received = lax.all_to_all(
        jnp.concatenate([second_out, pending], axis=3), "pix", 0, 0, tiled=True
    )
    pending = inbound(1, received[..., :width_one])
    term = model_of(0, received[..., width_one:])
    returned = lax.all_to_all(pending, "pix", 0, 0, tiled=True)
    term = term + model_of(1, returned)
    model_rows = lax.psum_scatter(term, "mode", scatter_dimension=0, tiled=True)
    own_means = lax.dynamic_slice_in_dim(block_means, mode_index * own_rows, own_rows, 1)
    own_centered = jnp.concatenate(
        [
            frames[:, b * block_len : (b + 1) * block_len] - own_means[b][:, None]
            for b in range(blocks)
        ],
        axis=1,
    )
    return own_centered - model_rows


def solution(mesh):
    return jax.shard_map(
        local,
        mesh=mesh,
        in_specs=(P("mode", "pix"), P("mode", "pix"), P("pix"), P()),
        out_specs=P("mode", "pix"),
        check_vma=False,
    )
```

```python
import jax
import jax.numpy as jnp
from jax import lax
from jax.sharding import PartitionSpec as P

NA = 8
K_CHUNKS = 2


HIGHEST_PRECISION = lax.Precision.HIGHEST
PRODUCT_PRECISION = lax.Precision.HIGH


def butterfly_sum(value, axes, size):
    step = 1
    while step < size:
        pairs = [(i, i ^ step) for i in range(size)]
        value = value + lax.ppermute(value, axes, pairs)
        step *= 2
    return value


def local(frames, basis, annulus, truncation):
    own_rows, pix_dev = frames.shape
    groups = lax.axis_size("mode")
    parts = lax.axis_size("pix")
    total_frames = own_rows * groups
    blocks = annulus.shape[0]
    block_len = pix_dev // blocks
    modes_dev = basis.shape[0]
    gathered = lax.all_gather(frames, "mode", axis=0, tiled=True)
    mode_index = lax.axis_index("mode")
    onehot = (annulus[:, None] == jnp.arange(NA, dtype=jnp.int32)[None, :]).astype(jnp.float32)
    own_block_sums = jnp.stack(
        [jnp.sum(frames[:, b * block_len : (b + 1) * block_len], axis=1) for b in range(blocks)],
        axis=0,
    )
    own_sums = jnp.einsum("ba,bf->af", onehot, own_block_sums, precision=HIGHEST_PRECISION)
    frame_slot = (
        mode_index * own_rows + jnp.arange(own_rows, dtype=jnp.int32)
    )[:, None] == jnp.arange(total_frames, dtype=jnp.int32)[None, :]
    local_sums = jnp.einsum(
        "af,fg->ag", own_sums, frame_slot.astype(jnp.float32), precision=HIGHEST_PRECISION
    )
    first_group = (mode_index == 0).astype(jnp.float32)
    local_counts = jnp.sum(onehot, axis=0) * (block_len * first_group)
    own_slot = (
        lax.axis_index("pix") * blocks + jnp.arange(blocks, dtype=jnp.int32)
    )[:, None] == jnp.arange(parts * blocks, dtype=jnp.int32)[None, :]
    local_table = jnp.einsum(
        "ba,bc->ac", onehot, own_slot.astype(jnp.float32), precision=HIGHEST_PRECISION
    ) * first_group
    packed = butterfly_sum(
        jnp.concatenate([local_sums, local_counts[:, None], local_table], axis=1),
        ("pix", "mode"),
        parts * groups,
    )
    annulus_totals = packed[:, :total_frames]
    pixel_counts = packed[:, total_frames]
    every_onehot = packed[:, total_frames + 1 :].T
    mode_ids = mode_index * modes_dev + jnp.arange(modes_dev, dtype=jnp.int32)
    retained = (mode_ids[None, :] < truncation[:, None]).astype(jnp.float32)
    annulus_means = annulus_totals / pixel_counts[:, None]
    block_means = jnp.einsum("ba,af->bf", onehot, annulus_means, precision=HIGHEST_PRECISION)
    centered = [
        gathered[:, b * block_len : (b + 1) * block_len] - block_means[b][:, None]
        for b in range(blocks)
    ]
    same_annulus = jnp.einsum("ca,ba->cb", every_onehot, every_onehot, precision=HIGHEST_PRECISION)
    block_retained = jnp.einsum("ba,ak->bk", every_onehot, retained, precision=HIGHEST_PRECISION)
    rows_dev = total_frames // parts
    split = (modes_dev * 3 // 8) // 128 * 128 or modes_dev // 2
    bounds = [(0, split), (split, modes_dev)]
    pieces = [
        [basis[lo:hi, b * block_len : (b + 1) * block_len] for b in range(blocks)]
        for lo, hi in bounds
    ]

    def outbound(c):
        width = bounds[c][1] - bounds[c][0]
        per_block = jnp.stack(
            [
                jnp.dot(centered[b], pieces[c][b].T, precision=PRODUCT_PRECISION)
                for b in range(blocks)
            ],
            axis=0,
        )
        return per_block.reshape(blocks, parts, rows_dev, width).transpose(1, 0, 2, 3)

    def inbound(c, arrived):
        lo, hi = bounds[c]
        summed = jnp.einsum(
            "cb,bfk->cfk",
            same_annulus,
            arrived.reshape(parts * blocks, rows_dev, hi - lo),
            precision=HIGHEST_PRECISION,
        )
        outgoing = summed * block_retained[:, None, lo:hi]
        return outgoing.reshape(parts, blocks, rows_dev, hi - lo)

    def model_of(c, returned):
        width = bounds[c][1] - bounds[c][0]
        picked = returned.transpose(1, 0, 2, 3).reshape(blocks, total_frames, width)
        return jnp.concatenate(
            [jnp.dot(picked[b], pieces[c][b], precision=PRODUCT_PRECISION) for b in range(blocks)],
            axis=1,
        )

    arrived = lax.all_to_all(outbound(0), "pix", 0, 0, tiled=True)
    pending = inbound(0, arrived)
    second_out = outbound(1)
    width_one = bounds[1][1] - bounds[1][0]
    received = lax.all_to_all(
        jnp.concatenate([second_out, pending], axis=3), "pix", 0, 0, tiled=True
    )
    pending = inbound(1, received[..., :width_one])
    term = model_of(0, received[..., width_one:])
    returned = lax.all_to_all(pending, "pix", 0, 0, tiled=True)
    term = term + model_of(1, returned)
    model_rows = lax.psum_scatter(term, "mode", scatter_dimension=0, tiled=True)
    own_means = lax.dynamic_slice_in_dim(block_means, mode_index * own_rows, own_rows, 1)
    own_centered = jnp.concatenate(
        [
            frames[:, b * block_len : (b + 1) * block_len] - own_means[b][:, None]
            for b in range(blocks)
        ],
        axis=1,
    )
    return own_centered - model_rows


def solution(mesh):
    return jax.shard_map(
        local,
        mesh=mesh,
        in_specs=(P("mode", "pix"), P("mode", "pix"), P("pix"), P()),
        out_specs=P("mode", "pix"),
        check_vma=False,
    )
```
